256 devices in a mesh: row: 32 (over y, z), col: 8 (over x, core).
Axes of the slice: x: 4, y: 4, z: 8, core: 2. Of those that a mesh axis runs over, the one named last changes fastest.
Arguments:
- features: bfloat16 [8, 8192, 256], P('col', 'row'), may hold values from -6 to 6
- self_weight: bfloat16 [256, 256], replicated, may hold values from -0.375 to 0.375
- neighbour_weight: bfloat16 [256, 256], replicated, may hold values from -0.375 to 0.375
- bias_term: bfloat16 [256], replicated, may hold values from -3 to 3
- cotangent: bfloat16 [8, 8192, 256], P('col', 'row'), may hold values from -6 to 6
- tile_values: bfloat16 [32, 8, 64, 128, 128], P('row', 'col'), as said below
- tile_rows: int32 [32, 8, 64], P('row', 'col'), may hold values from 0 to 15, as said below
- tile_cols: int32 [32, 8, 64], P('row', 'col'), may hold values from 0 to 63
- tile_count: int32 [32, 8], P('row', 'col'), may hold values from 16 to 64, as said below
- reorder: int32 [8, 8192], P('col'), may hold values from 0 to 8191, each once within a row
Outputs:
- activation: bfloat16 [8, 8192, 256], P('col', 'row')
- grad_features: bfloat16 [8, 8192, 256], P('col', 'row')
- grad_self: float32 [256, 256], replicated
- grad_neighbour: float32 [256, 256], replicated
- grad_bias: float32 [256], replicated
The draws below stay inside these ranges and needn't reach their ends.
Inputs may be any that keep to these rules, and one draw needn't show every extreme that they name: `tile_values`: entries are zero or positive. On each device the 64 slots name distinct tiles (pairs of tile_rows and tile_cols). `tile_count`: some device uses all 64 slots in every draw.
All inputs are finite; a program needn't handle non-finite values.
Results may differ from the reference program's by a relative error of at most 0.0065.
Values may be sent and summed in bfloat16 or wider, within the bound.
No kernel may reach another device: no remote copies, remote signals or barrier semaphores. Data moves between devices by JAX's collectives and lax.ppermute only.
A program may use at most 64 MiB of HBM per device.

```python
import math
import jax
import jax.numpy as jnp
from jax import lax

F = 256
BLK = 128
TILES_DEV = 64
NPD = 256
COLSET = 8192
ROWSET = 2048
ROW_BLOCKS = 16
COL_BLOCKS = 64
NODES = 65536
N_ROW = 32
N_COL = 8


def tile_slots(key):
    device_keys = jax.random.split(jax.random.fold_in(key, 7), N_ROW * N_COL)
    slots = jax.vmap(lambda single: jax.random.permutation(single, ROW_BLOCKS * COL_BLOCKS)[:TILES_DEV])(device_keys)
    return slots.reshape(N_ROW, N_COL, TILES_DEV).astype(jnp.int32)


def draw_tile_rows(key, part):
    return (tile_slots(key) // COL_BLOCKS).astype(jnp.int32)


def draw_tile_cols(key, part):
    return (tile_slots(key) % COL_BLOCKS).astype(jnp.int32)


def draw_tile_count(key, part):
    key_divisor, key_chosen = jax.random.split(jax.random.fold_in(key, 5))
    divisor = jax.random.randint(key_divisor, (N_ROW * N_COL,), 1, 5)
    chosen = jax.random.randint(key_chosen, (), 0, N_ROW * N_COL)
    divisor = jnp.where(jnp.arange(N_ROW * N_COL) == chosen, 1, divisor)
    return (TILES_DEV // divisor).reshape(N_ROW, N_COL).astype(jnp.int32)


def draw_tile_values(key, part):
    device_keys = jax.random.split(jax.random.fold_in(key, 3), N_ROW * N_COL)
    shape = (TILES_DEV, BLK, BLK)

    def one_device(inputs):
        device_key, device_id = inputs
        key_mask, key_weight = jax.random.split(device_key)
        uniform_mask = jax.random.uniform(key_mask, shape, jnp.float32)
        col_id = (device_id % N_COL).astype(jnp.float32)
        rising = 1.0 + 2.0 * col_id / max(N_COL - 1, 1)
        weight_draw = jax.random.uniform(key_weight, shape, jnp.float32, 0.5, 1.5)
        return jnp.where(uniform_mask < 0.125, weight_draw * rising, 0.0).astype(jnp.bfloat16)
    values = lax.map(one_device, (device_keys, jnp.arange(N_ROW * N_COL, dtype=jnp.int32)))
    return values.reshape(N_ROW, N_COL, TILES_DEV, BLK, BLK)


def block_levels(key, shape, cuts, low, high):
    factor_of = 1.0
    for dim, blocks in cuts:
        heights = jax.random.uniform(jax.random.fold_in(jax.random.fold_in(key, 6), dim), (blocks,), jnp.float32, low / len(cuts), high / len(cuts))
        factor_of = factor_of * jnp.repeat(jnp.exp(heights), shape[dim] // blocks).reshape((-1,) + (1,) * (len(shape) - 1 - dim))
    return factor_of


def normal_values(key, dims, scale, bound, shards=(), held_as=jnp.bfloat16):
    entries = jax.random.normal(key, dims, jnp.float32) * scale
    if len(shards) > 0:
        entries = block_levels(key, dims, shards, -0.22, 0.18) * entries
    return jnp.clip(entries, min=-bound, max=bound).astype(held_as)


def setup_inputs(seed: int = 0) -> dict:
    keys = jax.random.split(jax.random.key(seed), 11)
    return {
        "features": normal_values(keys[0], (N_COL, COLSET, F), 1.0, 6.0, ((0, 8), (1, 32))),
        "self_weight": normal_values(keys[1], (F, F), F ** -0.5, 0.375),
        "neighbour_weight": normal_values(keys[2], (F, F), F ** -0.5, 0.375),
        "bias_term": normal_values(keys[3], (F,), 0.5, 3.0),
        "cotangent": normal_values(keys[4], (N_COL, COLSET, F), 1.0, 6.0, ((0, 8), (1, 32))),
        "tile_values": draw_tile_values(jax.random.fold_in(keys[10], 71), 0),
        "tile_rows": draw_tile_rows(jax.random.fold_in(keys[10], 71), 0),
        "tile_cols": draw_tile_cols(jax.random.fold_in(keys[10], 71), 0),
        "tile_count": draw_tile_count(jax.random.fold_in(keys[10], 71), 0),
        "reorder": jax.vmap(lambda own: jax.random.permutation(own, COLSET))(jax.random.split(keys[9], N_COL)).reshape((N_COL, COLSET)).astype(jnp.int32),
    }


def reference(features, self_weight, neighbour_weight, bias_term, cotangent, tile_values, tile_rows, tile_cols, tile_count, reorder):
    ordered = jnp.take_along_axis(features, reorder[:, :, None], axis=1)
    device_total = N_ROW * N_COL

    def forward_device(device_id, carry):
        sums, degrees = carry
        row_id = device_id // N_COL
        col_id = device_id % N_COL
        values = tile_values[row_id, col_id].astype(jnp.float32)
        rows_here = tile_rows[row_id, col_id]
        cols_here = tile_cols[row_id, col_id]
        live_mask = (jnp.arange(TILES_DEV, dtype=jnp.int32) < tile_count[row_id, col_id]).astype(jnp.float32)
        column_group = ordered[col_id].reshape(COL_BLOCKS, BLK, F)
        picked = column_group[cols_here].astype(jnp.float32)
        products = jnp.einsum('tab,tbf->taf', values, picked) * live_mask[:, None, None]
        added = jax.ops.segment_sum(products, rows_here, num_segments=ROW_BLOCKS).reshape(ROWSET, F)
        weights = lax.optimization_barrier(jnp.sum(values, axis=2)) * live_mask[:, None]
        degree_add = jax.ops.segment_sum(weights, rows_here, num_segments=ROW_BLOCKS).reshape(ROWSET)
        sums = sums.at[row_id].add(added)
        degrees = degrees.at[row_id].add(degree_add)
        return (sums, degrees)
    start_sums = jnp.zeros((N_ROW, ROWSET, F), jnp.float32)
    start_degrees = jnp.zeros((N_ROW, ROWSET), jnp.float32)
    sums, degrees = lax.fori_loop(0, device_total, forward_device, (start_sums, start_degrees))
    sums = sums.reshape(N_ROW, N_COL, NPD, F).transpose(1, 0, 2, 3).reshape(NODES, F)
    degrees = degrees.reshape(N_ROW, N_COL, NPD).transpose(1, 0, 2).reshape(NODES)
    rescale = lax.rsqrt(1.0 + degrees)
    aggregate = (sums * rescale[:, None]).astype(jnp.bfloat16)
    own_rows = ordered.reshape(NODES, F)
    preact = jnp.dot(own_rows, self_weight, preferred_element_type=jnp.float32)
    preact = preact + jnp.dot(aggregate, neighbour_weight, preferred_element_type=jnp.float32)
    preact = preact + bias_term.astype(jnp.float32)[None, :]
    sigmoid_value = jax.nn.sigmoid(preact)
    activation = (preact * sigmoid_value).astype(jnp.bfloat16)
    slope = sigmoid_value * (1.0 + preact * (1.0 - sigmoid_value))
    grad_pre = (cotangent.reshape(NODES, F).astype(jnp.float32) * slope).astype(jnp.bfloat16)
    spread = (jnp.dot(grad_pre, neighbour_weight.T, preferred_element_type=jnp.float32) * rescale[:, None]).astype(jnp.bfloat16)
    spread_rows = spread.reshape(N_COL, N_ROW, NPD, F).transpose(1, 0, 2, 3).reshape(N_ROW, ROW_BLOCKS, BLK, F)

    def backward_device(device_id, column_totals):
        row_id = device_id // N_COL
        col_id = device_id % N_COL
        values = tile_values[row_id, col_id].astype(jnp.float32)
        rows_here = tile_rows[row_id, col_id]
        cols_here = tile_cols[row_id, col_id]
        live_mask = (jnp.arange(TILES_DEV, dtype=jnp.int32) < tile_count[row_id, col_id]).astype(jnp.float32)
        picked = spread_rows[row_id][rows_here].astype(jnp.float32)
        terms = jnp.einsum('tab,taf->tbf', values, picked) * live_mask[:, None, None]
        added = jax.ops.segment_sum(terms, cols_here, num_segments=COL_BLOCKS)
        return column_totals.at[col_id].add(added)
    column_totals = lax.fori_loop(0, device_total, backward_device, jnp.zeros((N_COL, COL_BLOCKS, BLK, F), jnp.float32))
    self_grad = jnp.dot(grad_pre, self_weight.T, preferred_element_type=jnp.float32).reshape(N_COL, COLSET, F)
    tile_grad = column_totals.reshape(N_COL, COLSET, F) + self_grad
    inverse = jnp.argsort(reorder, axis=1).astype(jnp.int32)
    grad_features = jnp.take_along_axis(tile_grad, inverse[:, :, None], axis=1).astype(jnp.bfloat16)
    grad_scale = 1.0 / math.sqrt(NODES)
    grad_self = jnp.dot(own_rows.T, grad_pre, preferred_element_type=jnp.float32) * grad_scale
    grad_neighbour = jnp.dot(aggregate.T, grad_pre, preferred_element_type=jnp.float32) * grad_scale
    grad_bias = lax.optimization_barrier(jnp.sum(grad_pre.astype(jnp.float32), axis=0)) * grad_scale
    return (activation.reshape(N_COL, COLSET, F), grad_features, grad_self, grad_neighbour, grad_bias)
```

```python
import math

import jax
import jax.numpy as jnp
from jax import lax
from jax.sharding import PartitionSpec as P


def block_onehot(block_ids, block_total, live_mask):
    targets = jnp.arange(block_total, dtype=jnp.int32)
    return (block_ids[:, None] == targets[None, :]).astype(jnp.float32) * live_mask[:, None]


def on_device(
    features,
    self_weight,
    neighbour_weight,
    bias_term,
    cotangent,
    tile_values,
    tile_rows,
    tile_cols,
    tile_count,
    reorder,
):
    row_count = lax.axis_size("row")
    col_count = lax.axis_size("col")
    row_index = lax.axis_index("row")
    col_index = lax.axis_index("col")
    per_device = features.shape[1]
    feature_width = features.shape[2]
    slot_count = tile_values.shape[2]
    block_side = tile_values.shape[3]
    row_blocks = col_count * per_device // block_side
    col_blocks = row_count * per_device // block_side
    blocks = tile_values[0, 0]
    tile_row_ids = tile_rows[0, 0]
    tile_col_ids = tile_cols[0, 0]
    live_mask = (jnp.arange(slot_count, dtype=jnp.int32) < tile_count[0, 0]).astype(jnp.float32)
    row_pick = block_onehot(tile_row_ids, row_blocks, live_mask)
    column_selection = block_onehot(tile_col_ids, col_blocks, live_mask)
    order_here = reorder[0]
    group_extent = 32
    maximum_value = lax.Precision.HIGHEST
    contract_rows = (((0,), (0,)), ((), ()))
    contract_cols = (((1,), (1,)), ((), ()))
    row_weight = jnp.sum(blocks, axis=2, dtype=jnp.float32)
    degree_part = lax.dot_general(
        row_pick, row_weight, contract_rows, precision=maximum_value
    ).reshape(col_count, per_device)
    inverse = (
        jnp.zeros_like(order_here)
        .at[order_here]
        .set(jnp.arange(order_here.shape[0], dtype=jnp.int32))
    )
    gathered = lax.all_gather(features, "row", axis=1, tiled=True)[0]
    gathered, inverse = lax.optimization_barrier((gathered, inverse))
    lookup = order_here.reshape(col_blocks, block_side)[tile_col_ids]
    partial_value = jnp.zeros((row_blocks, block_side, feature_width), jnp.float32)
    for start_shift in range(0, slot_count, group_extent):
        picked = gathered[lookup[start_shift : start_shift + group_extent]]
        products = jnp.einsum(
            "tab,tbf->taf",
            blocks[start_shift : start_shift + group_extent],
            picked,
            preferred_element_type=jnp.float32,
        )
        partial_value = partial_value + jnp.einsum(
            "tr,taf->raf",
            row_pick[start_shift : start_shift + group_extent],
            products,
            precision=maximum_value,
        )
    partial_value = partial_value.reshape(col_count, per_device, feature_width)
    degree_rows = jnp.zeros((col_count, 8, feature_width), jnp.float32)
    degree_rows = degree_rows.at[:, 0, :per_device].set(degree_part)
    partial_value = jnp.concatenate([partial_value, degree_rows], axis=1)
    reduced = lax.psum_scatter(partial_value, "col", scatter_dimension=0, tiled=True)[0]
    summed_result = reduced[:per_device]
    degree_own = reduced[per_device, :per_device]
    rescale = lax.rsqrt(1.0 + degree_own)
    aggregate = (summed_result * rescale[:, None]).astype(jnp.bfloat16)
    own_positions = lax.dynamic_slice_in_dim(order_here, row_index * per_device, per_device)
    own_rows = gathered[own_positions]
    preact = jnp.dot(own_rows, self_weight, preferred_element_type=jnp.float32)
    preact = preact + jnp.dot(aggregate, neighbour_weight, preferred_element_type=jnp.float32)
    preact = preact + bias_term.astype(jnp.float32)[None, :]
    sigmoid_value = jax.nn.sigmoid(preact)
    activation = (preact * sigmoid_value).astype(jnp.bfloat16)
    slope = sigmoid_value * (1.0 + preact * (1.0 - sigmoid_value))
    grad_pre = (cotangent[0].astype(jnp.float32) * slope).astype(jnp.bfloat16)
    bias_rows = jnp.zeros((8, feature_width), jnp.float32)
    bias_rows = bias_rows.at[0].set(jnp.sum(grad_pre.astype(jnp.float32), axis=0))
    weight_stack = jnp.concatenate(
        [
            lax.dot_general(own_rows, grad_pre, contract_rows, preferred_element_type=jnp.float32),
            lax.dot_general(aggregate, grad_pre, contract_rows, preferred_element_type=jnp.float32),
            bias_rows,
        ],
        axis=0,
    )
    weight_stack = lax.psum(weight_stack, ("row", "col"))
    weight_sums = (
        weight_stack[:feature_width],
        weight_stack[feature_width : 2 * feature_width],
        weight_stack[2 * feature_width],
    )
    grad_scale = 1.0 / math.sqrt(per_device * row_count * col_count)
    spread = (
        lax.dot_general(
            grad_pre, neighbour_weight, contract_cols, preferred_element_type=jnp.float32
        )
        * rescale[:, None]
    ).astype(jnp.bfloat16)
    spread_rows = lax.all_gather(spread[None], "col", axis=0, tiled=True).reshape(
        row_blocks, block_side, feature_width
    )
    col_part = jnp.zeros((col_blocks, block_side, feature_width), jnp.float32)
    for start_shift in range(0, slot_count, group_extent):
        spread_picked = spread_rows[tile_row_ids[start_shift : start_shift + group_extent]]
        backward_partials = jnp.einsum(
            "tab,taf->tbf",
            blocks[start_shift : start_shift + group_extent],
            spread_picked,
            preferred_element_type=jnp.float32,
        )
        col_part = col_part + jnp.einsum(
            "dy,dpe->ype",
            column_selection[start_shift : start_shift + group_extent],
            backward_partials,
            precision=maximum_value,
        )
    col_part = col_part.reshape(row_count * per_device, feature_width)
    self_grad = lax.dot_general(
        grad_pre, self_weight, contract_cols, preferred_element_type=jnp.float32
    )
    present_value = lax.dynamic_slice_in_dim(col_part, row_index * per_device, per_device, 0)
    col_part = lax.dynamic_update_slice_in_dim(
        col_part, present_value + self_grad, row_index * per_device, 0
    )
    initial = col_part[inverse]
    grad_features = lax.psum_scatter(initial[None], "row", scatter_dimension=1, tiled=True).astype(
        jnp.bfloat16
    )
    return (
        activation[None],
        grad_features,
        weight_sums[0] * grad_scale,
        weight_sums[1] * grad_scale,
        weight_sums[2] * grad_scale,
    )


def solution(mesh):
    return jax.shard_map(
        on_device,
        mesh=mesh,
        in_specs=(
            P("col", "row", None),
            P(),
            P(),
            P(),
            P("col", "row", None),
            P("row", "col", None, None, None),
            P("row", "col", None),
            P("row", "col", None),
            P("row", "col"),
            P("col", None),
        ),
        out_specs=(P("col", "row", None), P("col", "row", None), P(), P(), P()),
        check_vma=False,
    )
```

```python
import math

import jax
import jax.numpy as jnp
from jax import lax
from jax.sharding import Mesh, PartitionSpec as P


def block_onehot(block_ids, block_total, live_mask):
    targets = jnp.arange(block_total, dtype=jnp.int32)
    return (block_ids[:, None] == targets[None, :]).astype(jnp.float32) * live_mask[:, None]


def on_device(
    features,
    self_weight,
    neighbour_weight,
    bias_term,
    cotangent,
    tile_values,
    tile_rows,
    tile_cols,
    tile_count,
    reorder,
):
    row_count = lax.axis_size("y") * lax.axis_size("z")
    col_count = lax.axis_size("col")
    row_index = lax.axis_index("y") * lax.axis_size("z") + lax.axis_index("z")
    col_index = lax.axis_index("col")
    per_device = features.shape[1]
    feature_width = features.shape[2]
    slot_count = tile_values.shape[2]
    block_side = tile_values.shape[3]
    row_blocks = col_count * per_device // block_side
    col_blocks = row_count * per_device // block_side
    blocks = tile_values[0, 0]
    tile_row_ids = tile_rows[0, 0]
    tile_col_ids = tile_cols[0, 0]
    live_mask = (jnp.arange(slot_count, dtype=jnp.int32) < tile_count[0, 0]).astype(jnp.float32)
    row_pick = block_onehot(tile_row_ids, row_blocks, live_mask)
    column_selection = block_onehot(tile_col_ids, col_blocks, live_mask)
    order_here = reorder[0]
    group_extent = 32
    maximum_value = lax.Precision.HIGHEST
    contract_rows = (((0,), (0,)), ((), ()))
    contract_cols = (((1,), (1,)), ((), ()))
    row_weight = jnp.sum(blocks, axis=2, dtype=jnp.float32)
    degree_part = lax.dot_general(
        row_pick, row_weight, contract_rows, precision=maximum_value
    ).reshape(col_count, per_device)
    inverse = (
        jnp.zeros_like(order_here)
        .at[order_here]
        .set(jnp.arange(order_here.shape[0], dtype=jnp.int32))
    )
    gathered = lax.all_gather(features, ("y", "z"), axis=1, tiled=True)[0]
    gathered, inverse = lax.optimization_barrier((gathered, inverse))
    lookup = order_here.reshape(col_blocks, block_side)[tile_col_ids]
    partial_value = jnp.zeros((row_blocks, block_side, feature_width), jnp.float32)
    for start_shift in range(0, slot_count, group_extent):
        picked = gathered[lookup[start_shift : start_shift + group_extent]]
        products = jnp.einsum(
            "tab,tbf->taf",
            blocks[start_shift : start_shift + group_extent],
            picked,
            preferred_element_type=jnp.float32,
        )
        partial_value = partial_value + jnp.einsum(
            "tr,taf->raf",
            row_pick[start_shift : start_shift + group_extent],
            products,
            precision=maximum_value,
        )
    partial_value = partial_value.reshape(col_count, per_device, feature_width)
    degree_rows = jnp.zeros((col_count, 8, feature_width), jnp.float32)
    degree_rows = degree_rows.at[:, 0, :per_device].set(degree_part)
    partial_value = jnp.concatenate([partial_value, degree_rows], axis=1)
    reduced = lax.psum_scatter(partial_value, "col", scatter_dimension=0, tiled=True)[0]
    summed_result = reduced[:per_device]
    degree_own = reduced[per_device, :per_device]
    rescale = lax.rsqrt(1.0 + degree_own)
    aggregate = (summed_result * rescale[:, None]).astype(jnp.bfloat16)
    own_positions = lax.dynamic_slice_in_dim(order_here, row_index * per_device, per_device)
    own_rows = gathered[own_positions]
    preact = jnp.dot(own_rows, self_weight, preferred_element_type=jnp.float32)
    preact = preact + jnp.dot(aggregate, neighbour_weight, preferred_element_type=jnp.float32)
    preact = preact + bias_term.astype(jnp.float32)[None, :]
    sigmoid_value = jax.nn.sigmoid(preact)
    activation = (preact * sigmoid_value).astype(jnp.bfloat16)
    slope = sigmoid_value * (1.0 + preact * (1.0 - sigmoid_value))
    grad_pre = (cotangent[0].astype(jnp.float32) * slope).astype(jnp.bfloat16)
    bias_rows = jnp.zeros((8, feature_width), jnp.float32)
    bias_rows = bias_rows.at[0].set(jnp.sum(grad_pre.astype(jnp.float32), axis=0))
    weight_stack = jnp.concatenate(
        [
            lax.dot_general(own_rows, grad_pre, contract_rows, preferred_element_type=jnp.float32),
            lax.dot_general(aggregate, grad_pre, contract_rows, preferred_element_type=jnp.float32),
            bias_rows,
        ],
        axis=0,
    )
    weight_stack = lax.psum(weight_stack, "col")
    share_rows = -(-weight_stack.shape[0] // row_count)
    weight_stack = jnp.pad(
        weight_stack, ((0, share_rows * row_count - weight_stack.shape[0]), (0, 0))
    ).reshape(row_count, share_rows, feature_width)
    grad_scale = 1.0 / math.sqrt(per_device * row_count * col_count)
    spread = (
        lax.dot_general(
            grad_pre, neighbour_weight, contract_cols, preferred_element_type=jnp.float32
        )
        * rescale[:, None]
    ).astype(jnp.bfloat16)
    spread_rows = lax.all_gather(spread[None], "col", axis=0, tiled=True).reshape(
        row_blocks, block_side, feature_width
    )
    col_part = jnp.zeros((col_blocks, block_side, feature_width), jnp.float32)
    for start_shift in range(0, slot_count, group_extent):
        spread_picked = spread_rows[tile_row_ids[start_shift : start_shift + group_extent]]
        backward_partials = jnp.einsum(
            "tab,taf->tbf",
            blocks[start_shift : start_shift + group_extent],
            spread_picked,
            preferred_element_type=jnp.float32,
        )
        col_part = col_part + jnp.einsum(
            "dy,dpe->ype",
            column_selection[start_shift : start_shift + group_extent],
            backward_partials,
            precision=maximum_value,
        )
    col_part = col_part.reshape(row_count * per_device, feature_width)
    self_grad = lax.dot_general(
        grad_pre, self_weight, contract_cols, preferred_element_type=jnp.float32
    )
    present_value = lax.dynamic_slice_in_dim(col_part, row_index * per_device, per_device, 0)
    col_part = lax.dynamic_update_slice_in_dim(
        col_part, present_value + self_grad, row_index * per_device, 0
    )
    y_count = lax.axis_size("y")
    z_count = lax.axis_size("z")
    stage_order = inverse.reshape(y_count, z_count, per_device).transpose(1, 0, 2)
    initial = col_part[stage_order.reshape(-1)].reshape(z_count, y_count, per_device, feature_width)
    share_stage = weight_stack.reshape(y_count, z_count, share_rows, feature_width).transpose(1, 0, 2, 3)
    chunk_rows = -(-(per_device + share_rows) // 8) * 8
    share_stage = jnp.pad(
        share_stage, ((0, 0), (0, 0), (0, chunk_rows - per_device - share_rows), (0, 0))
    )
    initial = jnp.concatenate([initial, share_stage], axis=2)
    reduced_rows = lax.psum_scatter(initial, "z", scatter_dimension=0, tiled=True)[0]
    reduced_rows = lax.psum_scatter(reduced_rows, "y", scatter_dimension=0, tiled=True)[0]
    grad_features = reduced_rows[None, :per_device].astype(jnp.bfloat16)
    weight_share = reduced_rows[per_device : per_device + share_rows]
    weight_stack = lax.all_gather(weight_share, ("y", "z"), axis=0, tiled=True)
    weight_sums = (
        weight_stack[:feature_width],
        weight_stack[feature_width : 2 * feature_width],
        weight_stack[2 * feature_width],
    )
    return (
        activation[None],
        grad_features,
        weight_sums[0] * grad_scale,
        weight_sums[1] * grad_scale,
        weight_sums[2] * grad_scale,
    )


def torus_split(mesh):
    row_devices = mesh.devices[:, 0]
    try:
        z_count = len({device.coords[2] for device in row_devices})
    except (AttributeError, IndexError, TypeError):
        z_count = 8
    if row_devices.shape[0] % z_count:
        z_count = 1
    return z_count


def solution(mesh):
    z_count = torus_split(mesh)
    y_count = mesh.devices.shape[0] // z_count
    split_mesh = Mesh(mesh.devices.reshape(y_count, z_count, -1), ("y", "z", "col"))
    row = ("y", "z")
    return jax.shard_map(
        on_device,
        mesh=split_mesh,
        in_specs=(
            P("col", row, None),
            P(),
            P(),
            P(),
            P("col", row, None),
            P(row, "col", None, None, None),
            P(row, "col", None),
            P(row, "col", None),
            P(row, "col"),
            P("col", None),
        ),
        out_specs=(P("col", row, None), P("col", row, None), P(), P(), P()),
        check_vma=False,
    )
```

```python
import math

import jax
import jax.numpy as jnp
from jax import lax
from jax.sharding import Mesh, PartitionSpec as P


def block_onehot(block_ids, block_total, live_mask):
    targets = jnp.arange(block_total, dtype=jnp.int32)
    return (block_ids[:, None] == targets[None, :]).astype(jnp.float32) * live_mask[:, None]


def on_device(
    features,
    self_weight,
    neighbour_weight,
    bias_term,
    cotangent,
    tile_values,
    tile_rows,
    tile_cols,
    tile_count,
    reorder,
):
    row_count = lax.axis_size("y") * lax.axis_size("z")
    col_count = lax.axis_size("col")
    row_index = lax.axis_index("y") * lax.axis_size("z") + lax.axis_index("z")
    col_index = lax.axis_index("col")
    per_device = features.shape[1]
    feature_width = features.shape[2]
    slot_count = tile_values.shape[2]
    block_side = tile_values.shape[3]
    row_blocks = col_count * per_device // block_side
    col_blocks = row_count * per_device // block_side
    blocks = tile_values[0, 0]
    tile_row_ids = tile_rows[0, 0]
    tile_col_ids = tile_cols[0, 0]
    live_mask = (jnp.arange(slot_count, dtype=jnp.int32) < tile_count[0, 0]).astype(jnp.float32)
    row_pick = block_onehot(tile_row_ids, row_blocks, live_mask)
    column_selection = block_onehot(tile_col_ids, col_blocks, live_mask)
    order_here = reorder[0]
    group_extent = 32
    maximum_value = lax.Precision.HIGHEST
    contract_rows = (((0,), (0,)), ((), ()))
    contract_cols = (((1,), (1,)), ((), ()))
    row_weight = jnp.sum(blocks, axis=2, dtype=jnp.float32)
    degree_part = lax.dot_general(
        row_pick, row_weight, contract_rows, precision=maximum_value
    ).reshape(col_count, per_device)
    inverse = (
        jnp.zeros_like(order_here)
        .at[order_here]
        .set(jnp.arange(order_here.shape[0], dtype=jnp.int32))
    )
    gathered = lax.all_gather(features, ("y", "z"), axis=1, tiled=True)[0]
    gathered, inverse = lax.optimization_barrier((gathered, inverse))
    lookup = order_here.reshape(col_blocks, block_side)[tile_col_ids]
    partial_value = jnp.zeros((row_blocks, block_side, feature_width), jnp.float32)
    for start_shift in range(0, slot_count, group_extent):
        picked = gathered[lookup[start_shift : start_shift + group_extent]]
        products = jnp.einsum(
            "tab,tbf->taf",
            blocks[start_shift : start_shift + group_extent],
            picked,
            preferred_element_type=jnp.float32,
        )
        partial_value = partial_value + jnp.einsum(
            "tr,taf->raf",
            row_pick[start_shift : start_shift + group_extent],
            products,
            precision=maximum_value,
        )
    partial_value = partial_value.reshape(col_count, per_device, feature_width)
    degree_rows = jnp.zeros((col_count, 8, feature_width), jnp.float32)
    degree_rows = degree_rows.at[:, 0, :per_device].set(degree_part)
    partial_value = jnp.concatenate([partial_value, degree_rows], axis=1)
    reduced = lax.psum_scatter(partial_value, "col", scatter_dimension=0, tiled=True)[0]
    summed_result = reduced[:per_device]
    degree_own = reduced[per_device, :per_device]
    rescale = lax.rsqrt(1.0 + degree_own)
    aggregate = (summed_result * rescale[:, None]).astype(jnp.bfloat16)
    own_positions = lax.dynamic_slice_in_dim(order_here, row_index * per_device, per_device)
    own_rows = gathered[own_positions]
    preact = jnp.dot(own_rows, self_weight, preferred_element_type=jnp.float32)
    preact = preact + jnp.dot(aggregate, neighbour_weight, preferred_element_type=jnp.float32)
    preact = preact + bias_term.astype(jnp.float32)[None, :]
    sigmoid_value = jax.nn.sigmoid(preact)
    activation = (preact * sigmoid_value).astype(jnp.bfloat16)
    slope = sigmoid_value * (1.0 + preact * (1.0 - sigmoid_value))
    grad_pre = (cotangent[0].astype(jnp.float32) * slope).astype(jnp.bfloat16)
    grad_scale = 1.0 / math.sqrt(per_device * row_count * col_count)
    spread = (
        lax.dot_general(
            grad_pre, neighbour_weight, contract_cols, preferred_element_type=jnp.float32
        )
        * rescale[:, None]
    ).astype(jnp.bfloat16)
    spread_rows = lax.all_gather(spread[None], "col", axis=0, tiled=True).reshape(
        row_blocks, block_side, feature_width
    )
    bias_rows = jnp.zeros((8, feature_width), jnp.float32)
    bias_rows = bias_rows.at[0].set(jnp.sum(grad_pre.astype(jnp.float32), axis=0))
    weight_stack = jnp.concatenate(
        [
            lax.dot_general(own_rows, grad_pre, contract_rows, preferred_element_type=jnp.float32),
            lax.dot_general(aggregate, grad_pre, contract_rows, preferred_element_type=jnp.float32),
            bias_rows,
        ],
        axis=0,
    )
    weight_stack, spread_rows = lax.optimization_barrier((weight_stack, spread_rows))
    weight_stack = lax.psum(weight_stack, "col")
    share_rows = -(-weight_stack.shape[0] // row_count)
    weight_stack = jnp.pad(
        weight_stack, ((0, share_rows * row_count - weight_stack.shape[0]), (0, 0))
    ).reshape(row_count, share_rows, feature_width)
    col_part = jnp.zeros((col_blocks, block_side, feature_width), jnp.float32)
    for start_shift in range(0, slot_count, group_extent):
        spread_picked = spread_rows[tile_row_ids[start_shift : start_shift + group_extent]]
        backward_partials = jnp.einsum(
            "tab,taf->tbf",
            blocks[start_shift : start_shift + group_extent],
            spread_picked,
            preferred_element_type=jnp.float32,
        )
        col_part = col_part + jnp.einsum(
            "dy,dpe->ype",
            column_selection[start_shift : start_shift + group_extent],
            backward_partials,
            precision=maximum_value,
        )
    col_part = col_part.reshape(row_count * per_device, feature_width)
    self_grad = lax.dot_general(
        grad_pre, self_weight, contract_cols, preferred_element_type=jnp.float32
    )
    present_value = lax.dynamic_slice_in_dim(col_part, row_index * per_device, per_device, 0)
    col_part = lax.dynamic_update_slice_in_dim(
        col_part, present_value + self_grad, row_index * per_device, 0
    )
    y_count = lax.axis_size("y")
    z_count = lax.axis_size("z")
    stage_order = inverse.reshape(y_count, z_count, per_device).transpose(1, 0, 2)
    initial = col_part[stage_order.reshape(-1)].reshape(z_count, y_count, per_device, feature_width)
    share_stage = weight_stack.reshape(y_count, z_count, share_rows, feature_width).transpose(1, 0, 2, 3)
    chunk_rows = -(-(per_device + share_rows) // 8) * 8
    share_stage = jnp.pad(
        share_stage, ((0, 0), (0, 0), (0, chunk_rows - per_device - share_rows), (0, 0))
    )
    initial = jnp.concatenate([initial, share_stage], axis=2)
    reduced_rows = lax.psum_scatter(initial, "z", scatter_dimension=0, tiled=True)[0]
    reduced_rows = lax.psum_scatter(reduced_rows, "y", scatter_dimension=0, tiled=True)[0]
    grad_features = reduced_rows[None, :per_device].astype(jnp.bfloat16)
    weight_share = reduced_rows[per_device : per_device + share_rows]
    weight_stack = lax.all_gather(weight_share, "z", axis=0, tiled=True)
    weight_stack = lax.all_gather(weight_stack, "y", axis=0, tiled=True)
    weight_sums = (
        weight_stack[:feature_width],
        weight_stack[feature_width : 2 * feature_width],
        weight_stack[2 * feature_width],
    )
    return (
        activation[None],
        grad_features,
        weight_sums[0] * grad_scale,
        weight_sums[1] * grad_scale,
        weight_sums[2] * grad_scale,
    )


def torus_split(mesh):
    row_devices = mesh.devices[:, 0]
    try:
        z_count = len({device.coords[2] for device in row_devices})
    except (AttributeError, IndexError, TypeError):
        z_count = 8
    if row_devices.shape[0] % z_count:
        z_count = 1
    return z_count


def solution(mesh):
    z_count = torus_split(mesh)
    y_count = mesh.devices.shape[0] // z_count
    split_mesh = Mesh(mesh.devices.reshape(y_count, z_count, -1), ("y", "z", "col"))
    row = ("y", "z")
    return jax.shard_map(
        on_device,
        mesh=split_mesh,
        in_specs=(
            P("col", row, None),
            P(),
            P(),
            P(),
            P("col", row, None),
            P(row, "col", None, None, None),
            P(row, "col", None),
            P(row, "col", None),
            P(row, "col"),
            P("col", None),
        ),
        out_specs=(P("col", row, None), P("col", row, None), P(), P(), P()),
        check_vma=False,
    )
```

```python
import math

import jax
import jax.numpy as jnp
from jax import lax
from jax.experimental import pallas as pl
from jax.experimental.pallas import tpu as pltpu
from jax.sharding import Mesh, PartitionSpec as P


def tile_forward_kernel(rows_ref, cols_ref, count_ref, tiles_ref, x_ref, out_ref):
    slot = pl.program_id(0)
    side = tiles_ref.shape[1]

    @pl.when(slot == 0)
    def _():
        out_ref[...] = jnp.zeros_like(out_ref)

    @pl.when(slot < count_ref[0])
    def _():
        source = x_ref[pl.ds(pl.multiple_of(cols_ref[slot] * side, side), side), :]
        product = jnp.dot(tiles_ref[0], source, preferred_element_type=jnp.float32)
        target = pl.ds(pl.multiple_of(rows_ref[slot] * side, side), side)
        out_ref[target, :] = out_ref[target, :] + product


def tile_backward_kernel(rows_ref, cols_ref, count_ref, tiles_ref, s_ref, out_ref):
    slot = pl.program_id(0)
    side = tiles_ref.shape[1]

    @pl.when(slot == 0)
    def _():
        out_ref[...] = jnp.zeros_like(out_ref)

    @pl.when(slot < count_ref[0])
    def _():
        source = s_ref[pl.ds(pl.multiple_of(rows_ref[slot] * side, side), side), :]
        product = lax.dot_general(
            tiles_ref[0], source, (((0,), (0,)), ((), ())), preferred_element_type=jnp.float32
        )
        target = pl.ds(pl.multiple_of(cols_ref[slot] * side, side), side)
        out_ref[target, :] = out_ref[target, :] + product


def tile_product(kernel, tiles, rows, cols, count, source, out_rows, interpret=False):
    slots, side, _ = tiles.shape
    width = source.shape[1]
    tile_spec = pl.BlockSpec(
        (1, side, side), lambda t, r, c, n: (jnp.minimum(t, n[0] - 1), 0, 0)
    )
    grid_spec = pltpu.PrefetchScalarGridSpec(
        num_scalar_prefetch=3,
        grid=(slots,),
        in_specs=[tile_spec, pl.BlockSpec(source.shape, lambda t, r, c, n: (0, 0))],
        out_specs=pl.BlockSpec((out_rows, width), lambda t, r, c, n: (0, 0)),
    )
    return pl.pallas_call(
        kernel,
        grid_spec=grid_spec,
        out_shape=jax.ShapeDtypeStruct((out_rows, width), jnp.float32),
        interpret=interpret,
    )(rows, cols, count, tiles, source)


def block_onehot(block_ids, block_total, live_mask):
    targets = jnp.arange(block_total, dtype=jnp.int32)
    return (block_ids[:, None] == targets[None, :]).astype(jnp.float32) * live_mask[:, None]


def on_device(
    features,
    self_weight,
    neighbour_weight,
    bias_term,
    cotangent,
    tile_values,
    tile_rows,
    tile_cols,
    tile_count,
    reorder,
):
    row_count = lax.axis_size("y") * lax.axis_size("z")
    col_count = lax.axis_size("col")
    row_index = lax.axis_index("y") * lax.axis_size("z") + lax.axis_index("z")
    col_index = lax.axis_index("col")
    per_device = features.shape[1]
    feature_width = features.shape[2]
    slot_count = tile_values.shape[2]
    block_side = tile_values.shape[3]
    row_blocks = col_count * per_device // block_side
    col_blocks = row_count * per_device // block_side
    blocks = tile_values[0, 0]
    tile_row_ids = tile_rows[0, 0]
    tile_col_ids = tile_cols[0, 0]
    live_mask = (jnp.arange(slot_count, dtype=jnp.int32) < tile_count[0, 0]).astype(jnp.float32)
    row_pick = block_onehot(tile_row_ids, row_blocks, live_mask)
    order_here = reorder[0]
    maximum_value = lax.Precision.HIGHEST
    contract_rows = (((0,), (0,)), ((), ()))
    contract_cols = (((1,), (1,)), ((), ()))
    row_weight = jnp.sum(blocks, axis=2, dtype=jnp.float32)
    degree_part = lax.dot_general(
        row_pick, row_weight, contract_rows, precision=maximum_value
    ).reshape(col_count, per_device)
    inverse = (
        jnp.zeros_like(order_here)
        .at[order_here]
        .set(jnp.arange(order_here.shape[0], dtype=jnp.int32))
    )
    gathered = lax.all_gather(features, ("y", "z"), axis=1, tiled=True)[0]
    gathered, inverse = lax.optimization_barrier((gathered, inverse))
    ordered = gathered[order_here]
    live_count = tile_count[0].reshape(1)
    partial_value = tile_product(
        tile_forward_kernel, blocks, tile_row_ids, tile_col_ids, live_count, ordered,
        row_blocks * block_side,
    )
    partial_value = partial_value.reshape(col_count, per_device, feature_width)
    degree_rows = jnp.zeros((col_count, 8, feature_width), jnp.float32)
    degree_rows = degree_rows.at[:, 0, :per_device].set(degree_part)
    partial_value = jnp.concatenate([partial_value, degree_rows], axis=1)
    reduced = lax.psum_scatter(partial_value, "col", scatter_dimension=0, tiled=True)[0]
    summed_result = reduced[:per_device]
    degree_own = reduced[per_device, :per_device]
    rescale = lax.rsqrt(1.0 + degree_own)
    aggregate = (summed_result * rescale[:, None]).astype(jnp.bfloat16)
    own_positions = lax.dynamic_slice_in_dim(order_here, row_index * per_device, per_device)
    own_rows = gathered[own_positions]
    preact = jnp.dot(own_rows, self_weight, preferred_element_type=jnp.float32)
    preact = preact + jnp.dot(aggregate, neighbour_weight, preferred_element_type=jnp.float32)
    preact = preact + bias_term.astype(jnp.float32)[None, :]
    sigmoid_value = jax.nn.sigmoid(preact)
    activation = (preact * sigmoid_value).astype(jnp.bfloat16)
    slope = sigmoid_value * (1.0 + preact * (1.0 - sigmoid_value))
    grad_pre = (cotangent[0].astype(jnp.float32) * slope).astype(jnp.bfloat16)
    grad_scale = 1.0 / math.sqrt(per_device * row_count * col_count)
    spread = (
        lax.dot_general(
            grad_pre, neighbour_weight, contract_cols, preferred_element_type=jnp.float32
        )
        * rescale[:, None]
    ).astype(jnp.bfloat16)
    spread_rows = lax.all_gather(spread[None], "col", axis=0, tiled=True).reshape(
        row_blocks, block_side, feature_width
    )
    bias_rows = jnp.zeros((8, feature_width), jnp.float32)
    bias_rows = bias_rows.at[0].set(jnp.sum(grad_pre.astype(jnp.float32), axis=0))
    weight_stack = jnp.concatenate(
        [
            lax.dot_general(own_rows, grad_pre, contract_rows, preferred_element_type=jnp.float32),
            lax.dot_general(aggregate, grad_pre, contract_rows, preferred_element_type=jnp.float32),
            bias_rows,
        ],
        axis=0,
    )
    weight_stack, spread_rows = lax.optimization_barrier((weight_stack, spread_rows))
    weight_stack = lax.psum(weight_stack, "col")
    share_rows = -(-weight_stack.shape[0] // row_count)
    weight_stack = jnp.pad(
        weight_stack, ((0, share_rows * row_count - weight_stack.shape[0]), (0, 0))
    ).reshape(row_count, share_rows, feature_width)
    col_part = tile_product(
        tile_backward_kernel, blocks, tile_row_ids, tile_col_ids, live_count,
        spread_rows.reshape(row_blocks * block_side, feature_width), col_blocks * block_side,
    )
    col_part = col_part.reshape(row_count * per_device, feature_width)
    self_grad = lax.dot_general(
        grad_pre, self_weight, contract_cols, preferred_element_type=jnp.float32
    )
    present_value = lax.dynamic_slice_in_dim(col_part, row_index * per_device, per_device, 0)
    col_part = lax.dynamic_update_slice_in_dim(
        col_part, present_value + self_grad, row_index * per_device, 0
    )
    y_count = lax.axis_size("y")
    z_count = lax.axis_size("z")
    stage_order = inverse.reshape(y_count, z_count, per_device).transpose(1, 0, 2)
    initial = col_part[stage_order.reshape(-1)].reshape(z_count, y_count, per_device, feature_width)
    share_stage = weight_stack.reshape(y_count, z_count, share_rows, feature_width).transpose(1, 0, 2, 3)
    chunk_rows = -(-(per_device + share_rows) // 8) * 8
    share_stage = jnp.pad(
        share_stage, ((0, 0), (0, 0), (0, chunk_rows - per_device - share_rows), (0, 0))
    )
    initial = jnp.concatenate([initial, share_stage], axis=2)
    reduced_rows = lax.psum_scatter(initial, "z", scatter_dimension=0, tiled=True)[0]
    reduced_rows = lax.psum_scatter(reduced_rows, "y", scatter_dimension=0, tiled=True)[0]
    grad_features = reduced_rows[None, :per_device].astype(jnp.bfloat16)
    weight_share = reduced_rows[per_device : per_device + share_rows]
    weight_stack = lax.all_gather(weight_share, "z", axis=0, tiled=True)
    weight_stack = lax.all_gather(weight_stack, "y", axis=0, tiled=True)
    weight_sums = (
        weight_stack[:feature_width],
        weight_stack[feature_width : 2 * feature_width],
        weight_stack[2 * feature_width],
    )
    return (
        activation[None],
        grad_features,
        weight_sums[0] * grad_scale,
        weight_sums[1] * grad_scale,
        weight_sums[2] * grad_scale,
    )


def torus_split(mesh):
    row_devices = mesh.devices[:, 0]
    try:
        z_count = len({device.coords[2] for device in row_devices})
    except (AttributeError, IndexError, TypeError):
        z_count = 8
    if row_devices.shape[0] % z_count:
        z_count = 1
    return z_count


def solution(mesh):
    z_count = torus_split(mesh)
    y_count = mesh.devices.shape[0] // z_count
    split_mesh = Mesh(mesh.devices.reshape(y_count, z_count, -1), ("y", "z", "col"))
    row = ("y", "z")
    return jax.shard_map(
        on_device,
        mesh=split_mesh,
        in_specs=(
            P("col", row, None),
            P(),
            P(),
            P(),
            P("col", row, None),
            P(row, "col", None, None, None),
            P(row, "col", None),
            P(row, "col", None),
            P(row, "col"),
            P("col", None),
        ),
        out_specs=(P("col", row, None), P("col", row, None), P(), P(), P()),
        check_vma=False,
    )
```

```python
import math

import jax
import jax.numpy as jnp
from jax import lax
from jax.experimental import pallas as pl
from jax.experimental.pallas import tpu as pltpu
from jax.sharding import Mesh, PartitionSpec as P


def tile_forward_kernel(rows_ref, cols_ref, count_ref, tiles_ref, x_ref, out_ref):
    step = pl.program_id(0)
    group, side, _ = tiles_ref.shape

    @pl.when(step == 0)
    def _():
        out_ref[...] = jnp.zeros_like(out_ref)

    for offset in range(group):
        slot = step * group + offset

        @pl.when(slot < count_ref[0])
        def _():
            source = x_ref[pl.ds(pl.multiple_of(cols_ref[slot] * side, side), side), :]
            product = jnp.dot(tiles_ref[offset], source, preferred_element_type=jnp.float32)
            target = pl.ds(pl.multiple_of(rows_ref[slot] * side, side), side)
            out_ref[target, :] = out_ref[target, :] + product


def tile_backward_kernel(rows_ref, cols_ref, count_ref, tiles_ref, s_ref, out_ref):
    step = pl.program_id(0)
    group, side, _ = tiles_ref.shape

    @pl.when(step == 0)
    def _():
        out_ref[...] = jnp.zeros_like(out_ref)

    for offset in range(group):
        slot = step * group + offset

        @pl.when(slot < count_ref[0])
        def _():
            source = s_ref[pl.ds(pl.multiple_of(rows_ref[slot] * side, side), side), :]
            product = lax.dot_general(
                tiles_ref[offset], source, (((0,), (0,)), ((), ())),
                preferred_element_type=jnp.float32,
            )
            target = pl.ds(pl.multiple_of(cols_ref[slot] * side, side), side)
            out_ref[target, :] = out_ref[target, :] + product


def tile_product(kernel, tiles, rows, cols, count, source, out_rows, interpret=False):
    slots, side, _ = tiles.shape
    group = 8 if slots % 8 == 0 else 1
    width = source.shape[1]
    grid_spec = pltpu.PrefetchScalarGridSpec(
        num_scalar_prefetch=3,
        grid=(slots // group,),
        in_specs=[
            pl.BlockSpec((group, side, side), lambda s, r, c, n: (s, 0, 0)),
            pl.BlockSpec(source.shape, lambda s, r, c, n: (0, 0)),
        ],
        out_specs=pl.BlockSpec((out_rows, width), lambda s, r, c, n: (0, 0)),
    )
    return pl.pallas_call(
        kernel,
        grid_spec=grid_spec,
        out_shape=jax.ShapeDtypeStruct((out_rows, width), jnp.float32),
        interpret=interpret,
    )(rows, cols, count, tiles, source)


def block_onehot(block_ids, block_total, live_mask):
    targets = jnp.arange(block_total, dtype=jnp.int32)
    return (block_ids[:, None] == targets[None, :]).astype(jnp.float32) * live_mask[:, None]


def on_device(
    features,
    self_weight,
    neighbour_weight,
    bias_term,
    cotangent,
    tile_values,
    tile_rows,
    tile_cols,
    tile_count,
    reorder,
):
    row_count = lax.axis_size("y") * lax.axis_size("z")
    col_count = lax.axis_size("col")
    row_index = lax.axis_index("y") * lax.axis_size("z") + lax.axis_index("z")
    col_index = lax.axis_index("col")
    per_device = features.shape[1]
    feature_width = features.shape[2]
    slot_count = tile_values.shape[2]
    block_side = tile_values.shape[3]
    row_blocks = col_count * per_device // block_side
    col_blocks = row_count * per_device // block_side
    blocks = tile_values[0, 0]
    tile_row_ids = tile_rows[0, 0]
    tile_col_ids = tile_cols[0, 0]
    live_mask = (jnp.arange(slot_count, dtype=jnp.int32) < tile_count[0, 0]).astype(jnp.float32)
    row_pick = block_onehot(tile_row_ids, row_blocks, live_mask)
    order_here = reorder[0]
    maximum_value = lax.Precision.HIGHEST
    contract_rows = (((0,), (0,)), ((), ()))
    contract_cols = (((1,), (1,)), ((), ()))
    row_weight = jnp.sum(blocks, axis=2, dtype=jnp.float32)
    degree_part = lax.dot_general(
        row_pick, row_weight, contract_rows, precision=maximum_value
    ).reshape(col_count, per_device)
    inverse = (
        jnp.zeros_like(order_here)
        .at[order_here]
        .set(jnp.arange(order_here.shape[0], dtype=jnp.int32))
    )
    gathered = lax.all_gather(features, ("y", "z"), axis=1, tiled=True)[0]
    gathered, inverse = lax.optimization_barrier((gathered, inverse))
    ordered = gathered[order_here]
    live_count = tile_count[0].reshape(1)
    partial_value = tile_product(
        tile_forward_kernel, blocks, tile_row_ids, tile_col_ids, live_count, ordered,
        row_blocks * block_side,
    )
    partial_value = partial_value.reshape(col_count, per_device, feature_width)
    degree_rows = jnp.zeros((col_count, 8, feature_width), jnp.float32)
    degree_rows = degree_rows.at[:, 0, :per_device].set(degree_part)
    partial_value = jnp.concatenate([partial_value, degree_rows], axis=1)
    reduced = lax.psum_scatter(partial_value, "col", scatter_dimension=0, tiled=True)[0]
    summed_result = reduced[:per_device]
    degree_own = reduced[per_device, :per_device]
    rescale = lax.rsqrt(1.0 + degree_own)
    aggregate = (summed_result * rescale[:, None]).astype(jnp.bfloat16)
    own_positions = lax.dynamic_slice_in_dim(order_here, row_index * per_device, per_device)
    own_rows = gathered[own_positions]
    preact = jnp.dot(own_rows, self_weight, preferred_element_type=jnp.float32)
    preact = preact + jnp.dot(aggregate, neighbour_weight, preferred_element_type=jnp.float32)
    preact = preact + bias_term.astype(jnp.float32)[None, :]
    sigmoid_value = jax.nn.sigmoid(preact)
    activation = (preact * sigmoid_value).astype(jnp.bfloat16)
    slope = sigmoid_value * (1.0 + preact * (1.0 - sigmoid_value))
    grad_pre = (cotangent[0].astype(jnp.float32) * slope).astype(jnp.bfloat16)
    grad_scale = 1.0 / math.sqrt(per_device * row_count * col_count)
    spread = (
        lax.dot_general(
            grad_pre, neighbour_weight, contract_cols, preferred_element_type=jnp.float32
        )
        * rescale[:, None]
    ).astype(jnp.bfloat16)
    spread_rows = lax.all_gather(spread[None], "col", axis=0, tiled=True).reshape(
        row_blocks, block_side, feature_width
    )
    bias_rows = jnp.zeros((8, feature_width), jnp.float32)
    bias_rows = bias_rows.at[0].set(jnp.sum(grad_pre.astype(jnp.float32), axis=0))
    weight_stack = jnp.concatenate(
        [
            lax.dot_general(own_rows, grad_pre, contract_rows, preferred_element_type=jnp.float32),
            lax.dot_general(aggregate, grad_pre, contract_rows, preferred_element_type=jnp.float32),
            bias_rows,
        ],
        axis=0,
    )
    weight_stack, spread_rows = lax.optimization_barrier((weight_stack, spread_rows))
    weight_stack = lax.psum(weight_stack, "col")
    share_rows = -(-weight_stack.shape[0] // row_count)
    weight_stack = jnp.pad(
        weight_stack, ((0, share_rows * row_count - weight_stack.shape[0]), (0, 0))
    ).reshape(row_count, share_rows, feature_width)
    col_part = tile_product(
        tile_backward_kernel, blocks, tile_row_ids, tile_col_ids, live_count,
        spread_rows.reshape(row_blocks * block_side, feature_width), col_blocks * block_side,
    )
    col_part = col_part.reshape(row_count * per_device, feature_width)
    self_grad = lax.dot_general(
        grad_pre, self_weight, contract_cols, preferred_element_type=jnp.float32
    )
    present_value = lax.dynamic_slice_in_dim(col_part, row_index * per_device, per_device, 0)
    col_part = lax.dynamic_update_slice_in_dim(
        col_part, present_value + self_grad, row_index * per_device, 0
    )
    y_count = lax.axis_size("y")
    z_count = lax.axis_size("z")
    stage_order = inverse.reshape(y_count, z_count, per_device).transpose(1, 0, 2)
    initial = col_part[stage_order.reshape(-1)].reshape(z_count, y_count, per_device, feature_width)
    share_stage = weight_stack.reshape(y_count, z_count, share_rows, feature_width).transpose(1, 0, 2, 3)
    chunk_rows = -(-(per_device + share_rows) // 8) * 8
    share_stage = jnp.pad(
        share_stage, ((0, 0), (0, 0), (0, chunk_rows - per_device - share_rows), (0, 0))
    )
    initial = jnp.concatenate([initial, share_stage], axis=2)
    reduced_rows = lax.psum_scatter(initial, "z", scatter_dimension=0, tiled=True)[0]
    reduced_rows = lax.psum_scatter(reduced_rows, "y", scatter_dimension=0, tiled=True)[0]
    grad_features = reduced_rows[None, :per_device].astype(jnp.bfloat16)
    weight_share = reduced_rows[per_device : per_device + share_rows]
    weight_stack = lax.all_gather(weight_share, "z", axis=0, tiled=True)
    weight_stack = lax.all_gather(weight_stack, "y", axis=0, tiled=True)
    weight_sums = (
        weight_stack[:feature_width],
        weight_stack[feature_width : 2 * feature_width],
        weight_stack[2 * feature_width],
    )
    return (
        activation[None],
        grad_features,
        weight_sums[0] * grad_scale,
        weight_sums[1] * grad_scale,
        weight_sums[2] * grad_scale,
    )


def torus_split(mesh):
    row_devices = mesh.devices[:, 0]
    try:
        z_count = len({device.coords[2] for device in row_devices})
    except (AttributeError, IndexError, TypeError):
        z_count = 8
    if row_devices.shape[0] % z_count:
        z_count = 1
    return z_count


def solution(mesh):
    z_count = torus_split(mesh)
    y_count = mesh.devices.shape[0] // z_count
    split_mesh = Mesh(mesh.devices.reshape(y_count, z_count, -1), ("y", "z", "col"))
    row = ("y", "z")
    return jax.shard_map(
        on_device,
        mesh=split_mesh,
        in_specs=(
            P("col", row, None),
            P(),
            P(),
            P(),
            P("col", row, None),
            P(row, "col", None, None, None),
            P(row, "col", None),
            P(row, "col", None),
            P(row, "col"),
            P("col", None),
        ),
        out_specs=(P("col", row, None), P("col", row, None), P(), P(), P()),
        check_vma=False,
    )
```

```python
import math

import jax
import jax.numpy as jnp
from jax import lax
from jax.experimental import pallas as pl
from jax.experimental.pallas import tpu as pltpu
from jax.sharding import Mesh, PartitionSpec as P


def tile_forward_kernel(rows_ref, cols_ref, count_ref, tiles_ref, x_ref, out_ref):
    step = pl.program_id(0)
    group, side, _ = tiles_ref.shape

    @pl.when(step == 0)
    def _():
        out_ref[...] = jnp.zeros_like(out_ref)

    for offset in range(group):
        slot = step * group + offset

        @pl.when(slot < count_ref[0])
        def _():
            source = x_ref[pl.ds(pl.multiple_of(cols_ref[slot] * side, side), side), :]
            product = jnp.dot(tiles_ref[offset], source, preferred_element_type=jnp.float32)
            target = pl.ds(pl.multiple_of(rows_ref[slot] * side, side), side)
            out_ref[target, :] = out_ref[target, :] + product


def tile_backward_kernel(rows_ref, cols_ref, count_ref, tiles_ref, s_ref, out_ref):
    step = pl.program_id(0)
    group, side, _ = tiles_ref.shape

    @pl.when(step == 0)
    def _():
        out_ref[...] = jnp.zeros_like(out_ref)

    for offset in range(group):
        slot = step * group + offset

        @pl.when(slot < count_ref[0])
        def _():
            source = s_ref[pl.ds(pl.multiple_of(rows_ref[slot] * side, side), side), :]
            product = lax.dot_general(
                tiles_ref[offset], source, (((0,), (0,)), ((), ())),
                preferred_element_type=jnp.float32,
            )
            target = pl.ds(pl.multiple_of(cols_ref[slot] * side, side), side)
            out_ref[target, :] = out_ref[target, :] + product


def tile_product(kernel, tiles, rows, cols, count, source, out_rows, interpret=False):
    slots, side, _ = tiles.shape
    group = 8 if slots % 8 == 0 else 1
    width = source.shape[1]
    grid_spec = pltpu.PrefetchScalarGridSpec(
        num_scalar_prefetch=3,
        grid=(slots // group,),
        in_specs=[
            pl.BlockSpec((group, side, side), lambda s, r, c, n: (s, 0, 0)),
            pl.BlockSpec(source.shape, lambda s, r, c, n: (0, 0)),
        ],
        out_specs=pl.BlockSpec((out_rows, width), lambda s, r, c, n: (0, 0)),
    )
    return pl.pallas_call(
        kernel,
        grid_spec=grid_spec,
        out_shape=jax.ShapeDtypeStruct((out_rows, width), jnp.float32),
        interpret=interpret,
    )(rows, cols, count, tiles, source)


def block_onehot(block_ids, block_total, live_mask):
    targets = jnp.arange(block_total, dtype=jnp.int32)
    return (block_ids[:, None] == targets[None, :]).astype(jnp.float32) * live_mask[:, None]


def on_device(
    features,
    self_weight,
    neighbour_weight,
    bias_term,
    cotangent,
    tile_values,
    tile_rows,
    tile_cols,
    tile_count,
    reorder,
):
    row_count = lax.axis_size("y") * lax.axis_size("z")
    col_count = lax.axis_size("x") * lax.axis_size("core")
    row_index = lax.axis_index("y") * lax.axis_size("z") + lax.axis_index("z")
    col_index = lax.axis_index("x") * lax.axis_size("core") + lax.axis_index("core")
    per_device = features.shape[1]
    feature_width = features.shape[2]
    slot_count = tile_values.shape[2]
    block_side = tile_values.shape[3]
    row_blocks = col_count * per_device // block_side
    col_blocks = row_count * per_device // block_side
    blocks = tile_values[0, 0]
    tile_row_ids = tile_rows[0, 0]
    tile_col_ids = tile_cols[0, 0]
    live_mask = (jnp.arange(slot_count, dtype=jnp.int32) < tile_count[0, 0]).astype(jnp.float32)
    row_pick = block_onehot(tile_row_ids, row_blocks, live_mask)
    order_here = reorder[0]
    maximum_value = lax.Precision.HIGHEST
    contract_rows = (((0,), (0,)), ((), ()))
    contract_cols = (((1,), (1,)), ((), ()))
    row_weight = jnp.sum(blocks, axis=2, dtype=jnp.float32)
    degree_part = lax.dot_general(
        row_pick, row_weight, contract_rows, precision=maximum_value
    ).reshape(col_count, per_device)
    inverse = (
        jnp.zeros_like(order_here)
        .at[order_here]
        .set(jnp.arange(order_here.shape[0], dtype=jnp.int32))
    )
    gathered = lax.all_gather(features, "z", axis=1, tiled=True)
    gathered = lax.all_gather(gathered, "y", axis=1, tiled=True)[0]
    gathered, inverse = lax.optimization_barrier((gathered, inverse))
    ordered = gathered[order_here]
    live_count = tile_count[0].reshape(1)
    partial_value = tile_product(
        tile_forward_kernel, blocks, tile_row_ids, tile_col_ids, live_count, ordered,
        row_blocks * block_side,
    )
    partial_value = partial_value.reshape(col_count, per_device, feature_width)
    degree_rows = jnp.zeros((col_count, 8, feature_width), jnp.float32)
    degree_rows = degree_rows.at[:, 0, :per_device].set(degree_part)
    partial_value = jnp.concatenate([partial_value, degree_rows], axis=1)
    x_count = lax.axis_size("x")
    core_count = lax.axis_size("core")
    partial_value = partial_value.reshape(x_count, core_count, *partial_value.shape[1:])
    partial_value = jnp.swapaxes(partial_value, 0, 1)
    reduced = lax.psum_scatter(partial_value, "core", scatter_dimension=0, tiled=True)[0]
    reduced = lax.psum_scatter(reduced, "x", scatter_dimension=0, tiled=True)[0]
    summed_result = reduced[:per_device]
    degree_own = reduced[per_device, :per_device]
    rescale = lax.rsqrt(1.0 + degree_own)
    aggregate = (summed_result * rescale[:, None]).astype(jnp.bfloat16)
    own_positions = lax.dynamic_slice_in_dim(order_here, row_index * per_device, per_device)
    own_rows = gathered[own_positions]
    preact = jnp.dot(own_rows, self_weight, preferred_element_type=jnp.float32)
    preact = preact + jnp.dot(aggregate, neighbour_weight, preferred_element_type=jnp.float32)
    preact = preact + bias_term.astype(jnp.float32)[None, :]
    sigmoid_value = jax.nn.sigmoid(preact)
    activation = (preact * sigmoid_value).astype(jnp.bfloat16)
    slope = sigmoid_value * (1.0 + preact * (1.0 - sigmoid_value))
    grad_pre = (cotangent[0].astype(jnp.float32) * slope).astype(jnp.bfloat16)
    grad_scale = 1.0 / math.sqrt(per_device * row_count * col_count)
    spread = (
        lax.dot_general(
            grad_pre, neighbour_weight, contract_cols, preferred_element_type=jnp.float32
        )
        * rescale[:, None]
    ).astype(jnp.bfloat16)
    spread_rows = lax.all_gather(spread[None], "core", axis=0, tiled=True)
    spread_rows = lax.all_gather(spread_rows, "x", axis=0, tiled=True).reshape(
        row_blocks, block_side, feature_width
    )
    bias_rows = jnp.zeros((8, feature_width), jnp.float32)
    bias_rows = bias_rows.at[0].set(jnp.sum(grad_pre.astype(jnp.float32), axis=0))
    weight_stack = jnp.concatenate(
        [
            lax.dot_general(own_rows, grad_pre, contract_rows, preferred_element_type=jnp.float32),
            lax.dot_general(aggregate, grad_pre, contract_rows, preferred_element_type=jnp.float32),
            bias_rows,
        ],
        axis=0,
    )
    weight_stack, spread_rows = lax.optimization_barrier((weight_stack, spread_rows))
    weight_stack = lax.psum(lax.psum(weight_stack, "core"), "x")
    share_rows = -(-weight_stack.shape[0] // row_count)
    weight_stack = jnp.pad(
        weight_stack, ((0, share_rows * row_count - weight_stack.shape[0]), (0, 0))
    ).reshape(row_count, share_rows, feature_width)
    col_part = tile_product(
        tile_backward_kernel, blocks, tile_row_ids, tile_col_ids, live_count,
        spread_rows.reshape(row_blocks * block_side, feature_width), col_blocks * block_side,
    )
    col_part = col_part.reshape(row_count * per_device, feature_width)
    self_grad = lax.dot_general(
        grad_pre, self_weight, contract_cols, preferred_element_type=jnp.float32
    )
    present_value = lax.dynamic_slice_in_dim(col_part, row_index * per_device, per_device, 0)
    col_part = lax.dynamic_update_slice_in_dim(
        col_part, present_value + self_grad, row_index * per_device, 0
    )
    y_count = lax.axis_size("y")
    z_count = lax.axis_size("z")
    stage_order = inverse.reshape(y_count, z_count, per_device).transpose(1, 0, 2)
    initial = col_part[stage_order.reshape(-1)].reshape(z_count, y_count, per_device, feature_width)
    share_stage = weight_stack.reshape(y_count, z_count, share_rows, feature_width).transpose(1, 0, 2, 3)
    chunk_rows = -(-(per_device + share_rows) // 8) * 8
    share_stage = jnp.pad(
        share_stage, ((0, 0), (0, 0), (0, chunk_rows - per_device - share_rows), (0, 0))
    )
    initial = jnp.concatenate([initial, share_stage], axis=2)
    reduced_rows = lax.psum_scatter(initial, "z", scatter_dimension=0, tiled=True)[0]
    reduced_rows = lax.psum_scatter(reduced_rows, "y", scatter_dimension=0, tiled=True)[0]
    grad_features = reduced_rows[None, :per_device].astype(jnp.bfloat16)
    weight_share = reduced_rows[per_device : per_device + share_rows]
    weight_stack = lax.all_gather(weight_share, "z", axis=0, tiled=True)
    weight_stack = lax.all_gather(weight_stack, "y", axis=0, tiled=True)
    weight_sums = (
        weight_stack[:feature_width],
        weight_stack[feature_width : 2 * feature_width],
        weight_stack[2 * feature_width],
    )
    return (
        activation[None],
        grad_features,
        weight_sums[0] * grad_scale,
        weight_sums[1] * grad_scale,
        weight_sums[2] * grad_scale,
    )


def torus_split(mesh):
    row_devices = mesh.devices[:, 0]
    try:
        z_count = len({device.coords[2] for device in row_devices})
    except (AttributeError, IndexError, TypeError):
        z_count = 8
    if row_devices.shape[0] % z_count:
        z_count = 1
    return z_count


def core_split(mesh):
    col_devices = mesh.devices[0, :]
    try:
        core_count = len({device.core_on_chip for device in col_devices})
    except (AttributeError, TypeError):
        core_count = 2
    if col_devices.shape[0] % core_count:
        core_count = 1
    return core_count


def solution(mesh):
    z_count = torus_split(mesh)
    y_count = mesh.devices.shape[0] // z_count
    core_count = core_split(mesh)
    x_count = mesh.devices.shape[1] // core_count
    split_mesh = Mesh(
        mesh.devices.reshape(y_count, z_count, x_count, core_count), ("y", "z", "x", "core")
    )
    row = ("y", "z")
    col = ("x", "core")
    return jax.shard_map(
        on_device,
        mesh=split_mesh,
        in_specs=(
            P(col, row, None),
            P(),
            P(),
            P(),
            P(col, row, None),
            P(row, col, None, None, None),
            P(row, col, None),
            P(row, col, None),
            P(row, col),
            P(col, None),
        ),
        out_specs=(P(col, row, None), P(col, row, None), P(), P(), P()),
        check_vma=False,
    )
```

```python
import math

import jax
import jax.numpy as jnp
from jax import lax
from jax.experimental import pallas as pl
from jax.experimental.pallas import tpu as pltpu
from jax.sharding import Mesh, PartitionSpec as P


def tile_forward_kernel(rows_ref, cols_ref, count_ref, tiles_ref, x_ref, out_ref):
    step = pl.program_id(0)
    group, side, _ = tiles_ref.shape

    @pl.when(step == 0)
    def _():
        out_ref[...] = jnp.zeros_like(out_ref)

    for offset in range(group):
        slot = step * group + offset

        @pl.when(slot < count_ref[0])
        def _():
            source = x_ref[pl.ds(pl.multiple_of(cols_ref[slot] * side, side), side), :]
            product = jnp.dot(tiles_ref[offset], source, preferred_element_type=jnp.float32)
            target = pl.ds(pl.multiple_of(rows_ref[slot] * side, side), side)
            out_ref[target, :] = out_ref[target, :] + product


def tile_backward_kernel(rows_ref, cols_ref, count_ref, tiles_ref, s_ref, out_ref):
    step = pl.program_id(0)
    group, side, _ = tiles_ref.shape

    @pl.when(step == 0)
    def _():
        out_ref[...] = jnp.zeros_like(out_ref)

    for offset in range(group):
        slot = step * group + offset

        @pl.when(slot < count_ref[0])
        def _():
            source = s_ref[pl.ds(pl.multiple_of(rows_ref[slot] * side, side), side), :]
            product = lax.dot_general(
                tiles_ref[offset], source, (((0,), (0,)), ((), ())),
                preferred_element_type=jnp.float32,
            )
            target = pl.ds(pl.multiple_of(cols_ref[slot] * side, side), side)
            out_ref[target, :] = out_ref[target, :] + product


def tile_product(kernel, tiles, rows, cols, count, source, out_rows, interpret=False):
    slots, side, _ = tiles.shape
    group = 8 if slots % 8 == 0 else 1
    width = source.shape[1]
    grid_spec = pltpu.PrefetchScalarGridSpec(
        num_scalar_prefetch=3,
        grid=(slots // group,),
        in_specs=[
            pl.BlockSpec((group, side, side), lambda s, r, c, n: (s, 0, 0)),
            pl.BlockSpec(source.shape, lambda s, r, c, n: (0, 0)),
        ],
        out_specs=pl.BlockSpec((out_rows, width), lambda s, r, c, n: (0, 0)),
    )
    return pl.pallas_call(
        kernel,
        grid_spec=grid_spec,
        out_shape=jax.ShapeDtypeStruct((out_rows, width), jnp.float32),
        interpret=interpret,
    )(rows, cols, count, tiles, source)


def exchange_sum(value, axis):
    size = lax.axis_size(axis)
    if size & (size - 1):
        return lax.psum(value, axis)
    distance = 1
    while distance < size:
        pairs = [(index, index ^ distance) for index in range(size)]
        value = value + lax.ppermute(value, axis, pairs)
        distance *= 2
    return value


def block_onehot(block_ids, block_total, live_mask):
    targets = jnp.arange(block_total, dtype=jnp.int32)
    return (block_ids[:, None] == targets[None, :]).astype(jnp.float32) * live_mask[:, None]


def on_device(
    features,
    self_weight,
    neighbour_weight,
    bias_term,
    cotangent,
    tile_values,
    tile_rows,
    tile_cols,
    tile_count,
    reorder,
):
    row_count = lax.axis_size("y") * lax.axis_size("z")
    col_count = lax.axis_size("col")
    row_index = lax.axis_index("y") * lax.axis_size("z") + lax.axis_index("z")
    col_index = lax.axis_index("col")
    per_device = features.shape[1]
    feature_width = features.shape[2]
    slot_count = tile_values.shape[2]
    block_side = tile_values.shape[3]
    row_blocks = col_count * per_device // block_side
    col_blocks = row_count * per_device // block_side
    blocks = tile_values[0, 0]
    tile_row_ids = tile_rows[0, 0]
    tile_col_ids = tile_cols[0, 0]
    live_mask = (jnp.arange(slot_count, dtype=jnp.int32) < tile_count[0, 0]).astype(jnp.float32)
    row_pick = block_onehot(tile_row_ids, row_blocks, live_mask)
    order_here = reorder[0]
    maximum_value = lax.Precision.HIGHEST
    contract_rows = (((0,), (0,)), ((), ()))
    contract_cols = (((1,), (1,)), ((), ()))
    row_weight = jnp.sum(blocks, axis=2, dtype=jnp.float32)
    degree_part = lax.dot_general(
        row_pick, row_weight, contract_rows, precision=maximum_value
    ).reshape(col_count, per_device)
    inverse = (
        jnp.zeros_like(order_here)
        .at[order_here]
        .set(jnp.arange(order_here.shape[0], dtype=jnp.int32))
    )
    gathered = lax.all_gather(features, ("y", "z"), axis=1, tiled=True)[0]
    gathered, inverse = lax.optimization_barrier((gathered, inverse))
    ordered = gathered[order_here]
    live_count = tile_count[0].reshape(1)
    partial_value = tile_product(
        tile_forward_kernel, blocks, tile_row_ids, tile_col_ids, live_count, ordered,
        row_blocks * block_side,
    )
    partial_value = partial_value.reshape(col_count, per_device, feature_width)
    degree_rows = jnp.zeros((col_count, 8, feature_width), jnp.float32)
    degree_rows = degree_rows.at[:, 0, :per_device].set(degree_part)
    partial_value = jnp.concatenate([partial_value, degree_rows], axis=1)
    reduced = lax.psum_scatter(partial_value, "col", scatter_dimension=0, tiled=True)[0]
    summed_result = reduced[:per_device]
    degree_own = reduced[per_device, :per_device]
    rescale = lax.rsqrt(1.0 + degree_own)
    aggregate = (summed_result * rescale[:, None]).astype(jnp.bfloat16)
    own_positions = lax.dynamic_slice_in_dim(order_here, row_index * per_device, per_device)
    own_rows = gathered[own_positions]
    preact = jnp.dot(own_rows, self_weight, preferred_element_type=jnp.float32)
    preact = preact + jnp.dot(aggregate, neighbour_weight, preferred_element_type=jnp.float32)
    preact = preact + bias_term.astype(jnp.float32)[None, :]
    sigmoid_value = jax.nn.sigmoid(preact)
    activation = (preact * sigmoid_value).astype(jnp.bfloat16)
    slope = sigmoid_value * (1.0 + preact * (1.0 - sigmoid_value))
    grad_pre = (cotangent[0].astype(jnp.float32) * slope).astype(jnp.bfloat16)
    grad_scale = 1.0 / math.sqrt(per_device * row_count * col_count)
    spread = (
        lax.dot_general(
            grad_pre, neighbour_weight, contract_cols, preferred_element_type=jnp.float32
        )
        * rescale[:, None]
    ).astype(jnp.bfloat16)
    spread_rows = lax.all_gather(spread[None], "col", axis=0, tiled=True).reshape(
        row_blocks, block_side, feature_width
    )
    bias_rows = jnp.zeros((8, feature_width), jnp.float32)
    bias_rows = bias_rows.at[0].set(jnp.sum(grad_pre.astype(jnp.float32), axis=0))
    weight_stack = jnp.concatenate(
        [
            lax.dot_general(own_rows, grad_pre, contract_rows, preferred_element_type=jnp.float32),
            lax.dot_general(aggregate, grad_pre, contract_rows, preferred_element_type=jnp.float32),
            bias_rows,
        ],
        axis=0,
    )
    weight_stack, spread_rows = lax.optimization_barrier((weight_stack, spread_rows))
    weight_stack = lax.psum(weight_stack, "col")
    weight_stack = exchange_sum(weight_stack, "z")
    weight_stack = exchange_sum(weight_stack, "y")
    col_part = tile_product(
        tile_backward_kernel, blocks, tile_row_ids, tile_col_ids, live_count,
        spread_rows.reshape(row_blocks * block_side, feature_width), col_blocks * block_side,
    )
    col_part = col_part.reshape(row_count * per_device, feature_width)
    self_grad = lax.dot_general(
        grad_pre, self_weight, contract_cols, preferred_element_type=jnp.float32
    )
    present_value = lax.dynamic_slice_in_dim(col_part, row_index * per_device, per_device, 0)
    col_part = lax.dynamic_update_slice_in_dim(
        col_part, present_value + self_grad, row_index * per_device, 0
    )
    y_count = lax.axis_size("y")
    z_count = lax.axis_size("z")
    stage_order = inverse.reshape(y_count, z_count, per_device).transpose(1, 0, 2)
    initial = col_part[stage_order.reshape(-1)].reshape(z_count, y_count, per_device, feature_width)
    reduced_rows = lax.psum_scatter(initial, "z", scatter_dimension=0, tiled=True)[0]
    reduced_rows, weight_stack = lax.optimization_barrier((reduced_rows, weight_stack))
    reduced_rows = lax.psum_scatter(reduced_rows, "y", scatter_dimension=0, tiled=True)[0]
    grad_features = reduced_rows[None].astype(jnp.bfloat16)
    weight_sums = (
        weight_stack[:feature_width],
        weight_stack[feature_width : 2 * feature_width],
        weight_stack[2 * feature_width],
    )
    return (
        activation[None],
        grad_features,
        weight_sums[0] * grad_scale,
        weight_sums[1] * grad_scale,
        weight_sums[2] * grad_scale,
    )


def torus_split(mesh):
    row_devices = mesh.devices[:, 0]
    try:
        z_count = len({device.coords[2] for device in row_devices})
    except (AttributeError, IndexError, TypeError):
        z_count = 8
    if row_devices.shape[0] % z_count:
        z_count = 1
    return z_count


def solution(mesh):
    z_count = torus_split(mesh)
    y_count = mesh.devices.shape[0] // z_count
    split_mesh = Mesh(mesh.devices.reshape(y_count, z_count, -1), ("y", "z", "col"))
    row = ("y", "z")
    return jax.shard_map(
        on_device,
        mesh=split_mesh,
        in_specs=(
            P("col", row, None),
            P(),
            P(),
            P(),
            P("col", row, None),
            P(row, "col", None, None, None),
            P(row, "col", None),
            P(row, "col", None),
            P(row, "col"),
            P("col", None),
        ),
        out_specs=(P("col", row, None), P("col", row, None), P(), P(), P()),
        check_vma=False,
    )
```

```python
import math

import jax
import jax.numpy as jnp
from jax import lax
from jax.experimental import pallas as pl
from jax.experimental.pallas import tpu as pltpu
from jax.sharding import Mesh, PartitionSpec as P


def tile_forward_kernel(rows_ref, cols_ref, count_ref, tiles_ref, x_ref, out_ref):
    step = pl.program_id(0)
    group, side, _ = tiles_ref.shape

    @pl.when(step == 0)
    def _():
        out_ref[...] = jnp.zeros_like(out_ref)

    for offset in range(group):
        slot = step * group + offset

        @pl.when(slot < count_ref[0])
        def _():
            source = x_ref[pl.ds(pl.multiple_of(cols_ref[slot] * side, side), side), :]
            product = jnp.dot(tiles_ref[offset], source, preferred_element_type=jnp.float32)
            target = pl.ds(pl.multiple_of(rows_ref[slot] * side, side), side)
            out_ref[target, :] = out_ref[target, :] + product


def tile_backward_kernel(rows_ref, cols_ref, count_ref, tiles_ref, s_ref, out_ref):
    step = pl.program_id(0)
    group, side, _ = tiles_ref.shape

    @pl.when(step == 0)
    def _():
        out_ref[...] = jnp.zeros_like(out_ref)

    for offset in range(group):
        slot = step * group + offset

        @pl.when(slot < count_ref[0])
        def _():
            source = s_ref[pl.ds(pl.multiple_of(rows_ref[slot] * side, side), side), :]
            product = lax.dot_general(
                tiles_ref[offset], source, (((0,), (0,)), ((), ())),
                preferred_element_type=jnp.float32,
            )
            target = pl.ds(pl.multiple_of(cols_ref[slot] * side, side), side)
            out_ref[target, :] = out_ref[target, :] + product


def tile_product(kernel, tiles, rows, cols, count, source, out_rows, interpret=False):
    slots, side, _ = tiles.shape
    group = 8 if slots % 8 == 0 else 1
    width = source.shape[1]
    grid_spec = pltpu.PrefetchScalarGridSpec(
        num_scalar_prefetch=3,
        grid=(slots // group,),
        in_specs=[
            pl.BlockSpec((group, side, side), lambda s, r, c, n: (s, 0, 0)),
            pl.BlockSpec(source.shape, lambda s, r, c, n: (0, 0)),
        ],
        out_specs=pl.BlockSpec((out_rows, width), lambda s, r, c, n: (0, 0)),
    )
    return pl.pallas_call(
        kernel,
        grid_spec=grid_spec,
        out_shape=jax.ShapeDtypeStruct((out_rows, width), jnp.float32),
        interpret=interpret,
    )(rows, cols, count, tiles, source)


def exchange_sum(value, axis):
    size = lax.axis_size(axis)
    if size & (size - 1):
        return lax.psum(value, axis)
    distance = 1
    while distance < size:
        pairs = [(index, index ^ distance) for index in range(size)]
        value = value + lax.ppermute(value, axis, pairs)
        distance *= 2
    return value


def block_onehot(block_ids, block_total, live_mask):
    targets = jnp.arange(block_total, dtype=jnp.int32)
    return (block_ids[:, None] == targets[None, :]).astype(jnp.float32) * live_mask[:, None]


def on_device(
    features,
    self_weight,
    neighbour_weight,
    bias_term,
    cotangent,
    tile_values,
    tile_rows,
    tile_cols,
    tile_count,
    reorder,
):
    row_count = lax.axis_size("y") * lax.axis_size("z")
    col_count = lax.axis_size("col")
    row_index = lax.axis_index("y") * lax.axis_size("z") + lax.axis_index("z")
    col_index = lax.axis_index("col")
    per_device = features.shape[1]
    feature_width = features.shape[2]
    slot_count = tile_values.shape[2]
    block_side = tile_values.shape[3]
    row_blocks = col_count * per_device // block_side
    col_blocks = row_count * per_device // block_side
    blocks = tile_values[0, 0]
    tile_row_ids = tile_rows[0, 0]
    tile_col_ids = tile_cols[0, 0]
    live_mask = (jnp.arange(slot_count, dtype=jnp.int32) < tile_count[0, 0]).astype(jnp.float32)
    row_pick = block_onehot(tile_row_ids, row_blocks, live_mask)
    order_here = reorder[0]
    maximum_value = lax.Precision.HIGHEST
    contract_rows = (((0,), (0,)), ((), ()))
    contract_cols = (((1,), (1,)), ((), ()))
    row_weight = jnp.sum(blocks, axis=2, dtype=jnp.float32)
    degree_part = lax.dot_general(
        row_pick, row_weight, contract_rows, precision=maximum_value
    ).reshape(col_count, per_device)
    inverse = (
        jnp.zeros_like(order_here)
        .at[order_here]
        .set(jnp.arange(order_here.shape[0], dtype=jnp.int32))
    )
    gathered = lax.all_gather(features, ("y", "z"), axis=1, tiled=True)[0]
    gathered, inverse = lax.optimization_barrier((gathered, inverse))
    ordered = gathered[order_here]
    live_count = tile_count[0].reshape(1)
    partial_value = tile_product(
        tile_forward_kernel, blocks, tile_row_ids, tile_col_ids, live_count, ordered,
        row_blocks * block_side,
    )
    partial_value = partial_value.reshape(col_count, per_device, feature_width)
    degree_rows = jnp.zeros((col_count, 8, feature_width), jnp.float32)
    degree_rows = degree_rows.at[:, 0, :per_device].set(degree_part)
    partial_value = jnp.concatenate([partial_value, degree_rows], axis=1)
    reduced = lax.psum_scatter(partial_value, "col", scatter_dimension=0, tiled=True)[0]
    summed_result = reduced[:per_device]
    degree_own = reduced[per_device, :per_device]
    rescale = lax.rsqrt(1.0 + degree_own)
    aggregate = (summed_result * rescale[:, None]).astype(jnp.bfloat16)
    own_positions = lax.dynamic_slice_in_dim(order_here, row_index * per_device, per_device)
    own_rows = gathered[own_positions]
    preact = jnp.dot(own_rows, self_weight, preferred_element_type=jnp.float32)
    preact = preact + jnp.dot(aggregate, neighbour_weight, preferred_element_type=jnp.float32)
    preact = preact + bias_term.astype(jnp.float32)[None, :]
    sigmoid_value = jax.nn.sigmoid(preact)
    activation = (preact * sigmoid_value).astype(jnp.bfloat16)
    slope = sigmoid_value * (1.0 + preact * (1.0 - sigmoid_value))
    grad_pre = (cotangent[0].astype(jnp.float32) * slope).astype(jnp.bfloat16)
    grad_scale = 1.0 / math.sqrt(per_device * row_count * col_count)
    spread = (
        lax.dot_general(
            grad_pre, neighbour_weight, contract_cols, preferred_element_type=jnp.float32
        )
        * rescale[:, None]
    ).astype(jnp.bfloat16)
    spread_rows = lax.all_gather(spread[None], "col", axis=0, tiled=True).reshape(
        row_blocks, block_side, feature_width
    )
    bias_rows = jnp.zeros((8, feature_width), jnp.float32)
    bias_rows = bias_rows.at[0].set(jnp.sum(grad_pre.astype(jnp.float32), axis=0))
    weight_stack = jnp.concatenate(
        [
            lax.dot_general(own_rows, grad_pre, contract_rows, preferred_element_type=jnp.float32),
            lax.dot_general(aggregate, grad_pre, contract_rows, preferred_element_type=jnp.float32),
            bias_rows,
        ],
        axis=0,
    )
    weight_stack = exchange_sum(weight_stack, "col")
    weight_stack, spread_rows = lax.optimization_barrier((weight_stack, spread_rows))
    weight_stack = exchange_sum(weight_stack, "z")
    weight_stack = exchange_sum(weight_stack, "y")
    col_part = tile_product(
        tile_backward_kernel, blocks, tile_row_ids, tile_col_ids, live_count,
        spread_rows.reshape(row_blocks * block_side, feature_width), col_blocks * block_side,
    )
    col_part = col_part.reshape(row_count * per_device, feature_width)
    self_grad = lax.dot_general(
        grad_pre, self_weight, contract_cols, preferred_element_type=jnp.float32
    )
    present_value = lax.dynamic_slice_in_dim(col_part, row_index * per_device, per_device, 0)
    col_part = lax.dynamic_update_slice_in_dim(
        col_part, present_value + self_grad, row_index * per_device, 0
    )
    y_count = lax.axis_size("y")
    z_count = lax.axis_size("z")
    stage_order = inverse.reshape(y_count, z_count, per_device).transpose(1, 0, 2)
    initial = col_part[stage_order.reshape(-1)].reshape(z_count, y_count, per_device, feature_width)
    reduced_rows = lax.psum_scatter(initial, "z", scatter_dimension=0, tiled=True)[0]
    reduced_rows, weight_stack = lax.optimization_barrier((reduced_rows, weight_stack))
    reduced_rows = lax.psum_scatter(reduced_rows, "y", scatter_dimension=0, tiled=True)[0]
    grad_features = reduced_rows[None].astype(jnp.bfloat16)
    weight_sums = (
        weight_stack[:feature_width],
        weight_stack[feature_width : 2 * feature_width],
        weight_stack[2 * feature_width],
    )
    return (
        activation[None],
        grad_features,
        weight_sums[0] * grad_scale,
        weight_sums[1] * grad_scale,
        weight_sums[2] * grad_scale,
    )


def torus_split(mesh):
    row_devices = mesh.devices[:, 0]
    try:
        z_count = len({device.coords[2] for device in row_devices})
    except (AttributeError, IndexError, TypeError):
        z_count = 8
    if row_devices.shape[0] % z_count:
        z_count = 1
    return z_count


def solution(mesh):
    z_count = torus_split(mesh)
    y_count = mesh.devices.shape[0] // z_count
    split_mesh = Mesh(mesh.devices.reshape(y_count, z_count, -1), ("y", "z", "col"))
    row = ("y", "z")
    return jax.shard_map(
        on_device,
        mesh=split_mesh,
        in_specs=(
            P("col", row, None),
            P(),
            P(),
            P(),
            P("col", row, None),
            P(row, "col", None, None, None),
            P(row, "col", None),
            P(row, "col", None),
            P(row, "col"),
            P("col", None),
        ),
        out_specs=(P("col", row, None), P("col", row, None), P(), P(), P()),
        check_vma=False,
    )
```

```python
import math

import jax
import jax.numpy as jnp
from jax import lax
from jax.experimental import pallas as pl
from jax.experimental.pallas import tpu as pltpu
from jax.sharding import Mesh, PartitionSpec as P


def tile_forward_kernel(rows_ref, cols_ref, count_ref, tiles_ref, x_ref, out_ref):
    step = pl.program_id(0)
    group, side, _ = tiles_ref.shape

    @pl.when(step == 0)
    def _():
        out_ref[...] = jnp.zeros_like(out_ref)

    for offset in range(group):
        slot = step * group + offset

        @pl.when(slot < count_ref[0])
        def _():
            source = x_ref[pl.ds(pl.multiple_of(cols_ref[slot] * side, side), side), :]
            product = jnp.dot(tiles_ref[offset], source, preferred_element_type=jnp.float32)
            target = pl.ds(pl.multiple_of(rows_ref[slot] * side, side), side)
            out_ref[target, :] = out_ref[target, :] + product


def tile_backward_kernel(rows_ref, cols_ref, count_ref, tiles_ref, s_ref, out_ref):
    step = pl.program_id(0)
    group, side, _ = tiles_ref.shape

    @pl.when(step == 0)
    def _():
        out_ref[...] = jnp.zeros_like(out_ref)

    for offset in range(group):
        slot = step * group + offset

        @pl.when(slot < count_ref[0])
        def _():
            source = s_ref[pl.ds(pl.multiple_of(rows_ref[slot] * side, side), side), :]
            product = lax.dot_general(
                tiles_ref[offset], source, (((0,), (0,)), ((), ())),
                preferred_element_type=jnp.float32,
            )
            target = pl.ds(pl.multiple_of(cols_ref[slot] * side, side), side)
            out_ref[target, :] = out_ref[target, :] + product


def tile_product(kernel, tiles, rows, cols, count, source, out_rows, interpret=False):
    slots, side, _ = tiles.shape
    group = 8 if slots % 8 == 0 else 1
    width = source.shape[1]
    grid_spec = pltpu.PrefetchScalarGridSpec(
        num_scalar_prefetch=3,
        grid=(slots // group,),
        in_specs=[
            pl.BlockSpec((group, side, side), lambda s, r, c, n: (s, 0, 0)),
            pl.BlockSpec(source.shape, lambda s, r, c, n: (0, 0)),
        ],
        out_specs=pl.BlockSpec((out_rows, width), lambda s, r, c, n: (0, 0)),
    )
    return pl.pallas_call(
        kernel,
        grid_spec=grid_spec,
        out_shape=jax.ShapeDtypeStruct((out_rows, width), jnp.float32),
        interpret=interpret,
    )(rows, cols, count, tiles, source)


def exchange_sum(value, axis):
    size = lax.axis_size(axis)
    if size & (size - 1):
        return lax.psum(value, axis)
    distance = 1
    while distance < size:
        pairs = [(index, index ^ distance) for index in range(size)]
        value = value + lax.ppermute(value, axis, pairs)
        distance *= 2
    return value


def block_onehot(block_ids, block_total, live_mask):
    targets = jnp.arange(block_total, dtype=jnp.int32)
    return (block_ids[:, None] == targets[None, :]).astype(jnp.float32) * live_mask[:, None]


def on_device(
    features,
    self_weight,
    neighbour_weight,
    bias_term,
    cotangent,
    tile_values,
    tile_rows,
    tile_cols,
    tile_count,
    reorder,
):
    row_count = lax.axis_size("y") * lax.axis_size("z")
    col_count = lax.axis_size("col")
    row_index = lax.axis_index("y") * lax.axis_size("z") + lax.axis_index("z")
    col_index = lax.axis_index("col")
    per_device = features.shape[1]
    feature_width = features.shape[2]
    slot_count = tile_values.shape[2]
    block_side = tile_values.shape[3]
    row_blocks = col_count * per_device // block_side
    col_blocks = row_count * per_device // block_side
    blocks = tile_values[0, 0]
    tile_row_ids = tile_rows[0, 0]
    tile_col_ids = tile_cols[0, 0]
    live_mask = (jnp.arange(slot_count, dtype=jnp.int32) < tile_count[0, 0]).astype(jnp.float32)
    row_pick = block_onehot(tile_row_ids, row_blocks, live_mask)
    order_here = reorder[0]
    maximum_value = lax.Precision.HIGHEST
    contract_rows = (((0,), (0,)), ((), ()))
    contract_cols = (((1,), (1,)), ((), ()))
    row_weight = jnp.sum(blocks, axis=2, dtype=jnp.float32)
    degree_part = lax.dot_general(
        row_pick, row_weight, contract_rows, precision=maximum_value
    ).reshape(col_count, per_device)
    inverse = (
        jnp.zeros_like(order_here)
        .at[order_here]
        .set(jnp.arange(order_here.shape[0], dtype=jnp.int32))
    )
    gathered = lax.all_gather(features, ("y", "z"), axis=1, tiled=True)[0]
    gathered, inverse = lax.optimization_barrier((gathered, inverse))
    ordered = gathered[order_here]
    live_count = tile_count[0].reshape(1)
    partial_value = tile_product(
        tile_forward_kernel, blocks, tile_row_ids, tile_col_ids, live_count, ordered,
        row_blocks * block_side,
    )
    partial_value = partial_value.reshape(col_count, per_device, feature_width)
    degree_rows = jnp.zeros((col_count, 8, feature_width), jnp.float32)
    degree_rows = degree_rows.at[:, 0, :per_device].set(degree_part)
    partial_value = jnp.concatenate([partial_value, degree_rows], axis=1)
    reduced = lax.psum_scatter(partial_value, "col", scatter_dimension=0, tiled=True)[0]
    summed_result = reduced[:per_device]
    degree_own = reduced[per_device, :per_device]
    rescale = lax.rsqrt(1.0 + degree_own)
    aggregate = (summed_result * rescale[:, None]).astype(jnp.bfloat16)
    own_positions = lax.dynamic_slice_in_dim(order_here, row_index * per_device, per_device)
    own_rows = gathered[own_positions]
    preact = jnp.dot(own_rows, self_weight, preferred_element_type=jnp.float32)
    preact = preact + jnp.dot(aggregate, neighbour_weight, preferred_element_type=jnp.float32)
    preact = preact + bias_term.astype(jnp.float32)[None, :]
    sigmoid_value = jax.nn.sigmoid(preact)
    activation = (preact * sigmoid_value).astype(jnp.bfloat16)
    slope = sigmoid_value * (1.0 + preact * (1.0 - sigmoid_value))
    grad_pre = (cotangent[0].astype(jnp.float32) * slope).astype(jnp.bfloat16)
    grad_scale = 1.0 / math.sqrt(per_device * row_count * col_count)
    spread = (
        lax.dot_general(
            grad_pre, neighbour_weight, contract_cols, preferred_element_type=jnp.float32
        )
        * rescale[:, None]
    ).astype(jnp.bfloat16)
    spread_rows = lax.all_gather(spread[None], "col", axis=0, tiled=True).reshape(
        row_blocks, block_side, feature_width
    )
    bias_rows = jnp.zeros((8, feature_width), jnp.float32)
    bias_rows = bias_rows.at[0].set(jnp.sum(grad_pre.astype(jnp.float32), axis=0))
    weight_stack = jnp.concatenate(
        [
            lax.dot_general(own_rows, grad_pre, contract_rows, preferred_element_type=jnp.float32),
            lax.dot_general(aggregate, grad_pre, contract_rows, preferred_element_type=jnp.float32),
            bias_rows,
        ],
        axis=0,
    )
    weight_stack = exchange_sum(weight_stack, "col")
    weight_stack, spread_rows = lax.optimization_barrier((weight_stack, spread_rows))
    weight_stack = exchange_sum(weight_stack, "y")
    col_part = tile_product(
        tile_backward_kernel, blocks, tile_row_ids, tile_col_ids, live_count,
        spread_rows.reshape(row_blocks * block_side, feature_width), col_blocks * block_side,
    )
    col_part = col_part.reshape(row_count * per_device, feature_width)
    self_grad = lax.dot_general(
        grad_pre, self_weight, contract_cols, preferred_element_type=jnp.float32
    )
    present_value = lax.dynamic_slice_in_dim(col_part, row_index * per_device, per_device, 0)
    col_part = lax.dynamic_update_slice_in_dim(
        col_part, present_value + self_grad, row_index * per_device, 0
    )
    y_count = lax.axis_size("y")
    z_count = lax.axis_size("z")
    stage_order = inverse.reshape(y_count, z_count, per_device).transpose(1, 0, 2)
    initial = col_part[stage_order.reshape(-1)].reshape(z_count, y_count, per_device, feature_width)
    reduced_rows = lax.psum_scatter(initial, "z", scatter_dimension=0, tiled=True)[0]
    reduced_rows, weight_stack = lax.optimization_barrier((reduced_rows, weight_stack))
    reduced_rows = lax.psum_scatter(reduced_rows, "y", scatter_dimension=0, tiled=True)[0]
    weight_stack = exchange_sum(weight_stack, "z")
    reduced_rows, weight_stack = lax.optimization_barrier((reduced_rows, weight_stack))
    grad_features = reduced_rows[None].astype(jnp.bfloat16)
    weight_sums = (
        weight_stack[:feature_width],
        weight_stack[feature_width : 2 * feature_width],
        weight_stack[2 * feature_width],
    )
    return (
        activation[None],
        grad_features,
        weight_sums[0] * grad_scale,
        weight_sums[1] * grad_scale,
        weight_sums[2] * grad_scale,
    )


def torus_split(mesh):
    row_devices = mesh.devices[:, 0]
    try:
        z_count = len({device.coords[2] for device in row_devices})
    except (AttributeError, IndexError, TypeError):
        z_count = 8
    if row_devices.shape[0] % z_count:
        z_count = 1
    return z_count


def solution(mesh):
    z_count = torus_split(mesh)
    y_count = mesh.devices.shape[0] // z_count
    split_mesh = Mesh(mesh.devices.reshape(y_count, z_count, -1), ("y", "z", "col"))
    row = ("y", "z")
    return jax.shard_map(
        on_device,
        mesh=split_mesh,
        in_specs=(
            P("col", row, None),
            P(),
            P(),
            P(),
            P("col", row, None),
            P(row, "col", None, None, None),
            P(row, "col", None),
            P(row, "col", None),
            P(row, "col"),
            P("col", None),
        ),
        out_specs=(P("col", row, None), P("col", row, None), P(), P(), P()),
        check_vma=False,
    )
```

```python
import math

import jax
import jax.numpy as jnp
from jax import lax
from jax.experimental import pallas as pl
from jax.experimental.pallas import tpu as pltpu
from jax.sharding import Mesh, PartitionSpec as P


def tile_forward_kernel(rows_ref, cols_ref, count_ref, tiles_ref, x_ref, out_ref):
    step = pl.program_id(0)
    group, side, _ = tiles_ref.shape

    @pl.when(step == 0)
    def _():
        out_ref[...] = jnp.zeros_like(out_ref)

    for offset in range(group):
        slot = step * group + offset

        @pl.when(slot < count_ref[0])
        def _():
            source = x_ref[pl.ds(pl.multiple_of(cols_ref[slot] * side, side), side), :]
            product = jnp.dot(tiles_ref[offset], source, preferred_element_type=jnp.float32)
            target = pl.ds(pl.multiple_of(rows_ref[slot] * side, side), side)
            out_ref[target, :] = out_ref[target, :] + product


def tile_backward_kernel(rows_ref, cols_ref, count_ref, tiles_ref, s_ref, out_ref):
    step = pl.program_id(0)
    group, side, _ = tiles_ref.shape

    @pl.when(step == 0)
    def _():
        out_ref[...] = jnp.zeros_like(out_ref)

    for offset in range(group):
        slot = step * group + offset

        @pl.when(slot < count_ref[0])
        def _():
            source = s_ref[pl.ds(pl.multiple_of(rows_ref[slot] * side, side), side), :]
            product = lax.dot_general(
                tiles_ref[offset], source, (((0,), (0,)), ((), ())),
                preferred_element_type=jnp.float32,
            )
            target = pl.ds(pl.multiple_of(cols_ref[slot] * side, side), side)
            out_ref[target, :] = out_ref[target, :] + product


def tile_product(kernel, tiles, rows, cols, count, source, out_rows, interpret=False):
    slots, side, _ = tiles.shape
    group = 8 if slots % 8 == 0 else 1
    width = source.shape[1]
    grid_spec = pltpu.PrefetchScalarGridSpec(
        num_scalar_prefetch=3,
        grid=(slots // group,),
        in_specs=[
            pl.BlockSpec((group, side, side), lambda s, r, c, n: (s, 0, 0)),
            pl.BlockSpec(source.shape, lambda s, r, c, n: (0, 0)),
        ],
        out_specs=pl.BlockSpec((out_rows, width), lambda s, r, c, n: (0, 0)),
    )
    return pl.pallas_call(
        kernel,
        grid_spec=grid_spec,
        out_shape=jax.ShapeDtypeStruct((out_rows, width), jnp.float32),
        interpret=interpret,
    )(rows, cols, count, tiles, source)


def exchange_sum(value, axis):
    size = lax.axis_size(axis)
    if size & (size - 1):
        return lax.psum(value, axis)
    distance = 1
    while distance < size:
        pairs = [(index, index ^ distance) for index in range(size)]
        value = value + lax.ppermute(value, axis, pairs)
        distance *= 2
    return value


def block_onehot(block_ids, block_total, live_mask):
    targets = jnp.arange(block_total, dtype=jnp.int32)
    return (block_ids[:, None] == targets[None, :]).astype(jnp.float32) * live_mask[:, None]


def on_device(
    features,
    self_weight,
    neighbour_weight,
    bias_term,
    cotangent,
    tile_values,
    tile_rows,
    tile_cols,
    tile_count,
    reorder,
):
    row_count = lax.axis_size("y") * lax.axis_size("z")
    col_count = lax.axis_size("col")
    row_index = lax.axis_index("y") * lax.axis_size("z") + lax.axis_index("z")
    col_index = lax.axis_index("col")
    per_device = features.shape[1]
    feature_width = features.shape[2]
    slot_count = tile_values.shape[2]
    block_side = tile_values.shape[3]
    row_blocks = col_count * per_device // block_side
    col_blocks = row_count * per_device // block_side
    blocks = tile_values[0, 0]
    tile_row_ids = tile_rows[0, 0]
    tile_col_ids = tile_cols[0, 0]
    live_mask = (jnp.arange(slot_count, dtype=jnp.int32) < tile_count[0, 0]).astype(jnp.float32)
    row_pick = block_onehot(tile_row_ids, row_blocks, live_mask)
    order_here = reorder[0]
    maximum_value = lax.Precision.HIGHEST
    contract_rows = (((0,), (0,)), ((), ()))
    contract_cols = (((1,), (1,)), ((), ()))
    row_weight = jnp.sum(blocks, axis=2, dtype=jnp.float32)
    degree_part = lax.dot_general(
        row_pick, row_weight, contract_rows, precision=maximum_value
    ).reshape(col_count, per_device)
    inverse = (
        jnp.zeros_like(order_here)
        .at[order_here]
        .set(jnp.arange(order_here.shape[0], dtype=jnp.int32))
    )
    gathered = lax.all_gather(features, ("y", "z"), axis=1, tiled=True)[0]
    gathered, inverse = lax.optimization_barrier((gathered, inverse))
    ordered = gathered[order_here]
    live_count = tile_count[0].reshape(1)
    partial_value = tile_product(
        tile_forward_kernel, blocks, tile_row_ids, tile_col_ids, live_count, ordered,
        row_blocks * block_side,
    )
    partial_value = partial_value.reshape(col_count, per_device, feature_width)
    degree_rows = jnp.zeros((col_count, 8, feature_width), jnp.float32)
    degree_rows = degree_rows.at[:, 0, :per_device].set(degree_part)
    partial_value = jnp.concatenate([partial_value, degree_rows], axis=1)
    reduced = lax.psum_scatter(partial_value, "col", scatter_dimension=0, tiled=True)[0]
    summed_result = reduced[:per_device]
    degree_own = reduced[per_device, :per_device]
    rescale = lax.rsqrt(1.0 + degree_own)
    aggregate = (summed_result * rescale[:, None]).astype(jnp.bfloat16)
    own_positions = lax.dynamic_slice_in_dim(order_here, row_index * per_device, per_device)
    own_rows = gathered[own_positions]
    preact = jnp.dot(own_rows, self_weight, preferred_element_type=jnp.float32)
    preact = preact + jnp.dot(aggregate, neighbour_weight, preferred_element_type=jnp.float32)
    preact = preact + bias_term.astype(jnp.float32)[None, :]
    sigmoid_value = jax.nn.sigmoid(preact)
    activation = (preact * sigmoid_value).astype(jnp.bfloat16)
    slope = sigmoid_value * (1.0 + preact * (1.0 - sigmoid_value))
    grad_pre = (cotangent[0].astype(jnp.float32) * slope).astype(jnp.bfloat16)
    grad_scale = 1.0 / math.sqrt(per_device * row_count * col_count)
    spread = (
        lax.dot_general(
            grad_pre, neighbour_weight, contract_cols, preferred_element_type=jnp.float32
        )
        * rescale[:, None]
    ).astype(jnp.bfloat16)
    spread_rows = lax.all_gather(spread[None], "col", axis=0, tiled=True).reshape(
        row_blocks, block_side, feature_width
    )
    bias_rows = jnp.zeros((8, feature_width), jnp.float32)
    bias_rows = bias_rows.at[0].set(jnp.sum(grad_pre.astype(jnp.float32), axis=0))
    weight_stack = jnp.concatenate(
        [
            lax.dot_general(own_rows, grad_pre, contract_rows, preferred_element_type=jnp.float32),
            lax.dot_general(aggregate, grad_pre, contract_rows, preferred_element_type=jnp.float32),
            bias_rows,
        ],
        axis=0,
    )
    weight_stack = exchange_sum(weight_stack, "col")
    weight_stack, spread_rows = lax.optimization_barrier((weight_stack, spread_rows))
    col_part = tile_product(
        tile_backward_kernel, blocks, tile_row_ids, tile_col_ids, live_count,
        spread_rows.reshape(row_blocks * block_side, feature_width), col_blocks * block_side,
    )
    col_part = col_part.reshape(row_count * per_device, feature_width)
    weight_stack, col_part = lax.optimization_barrier((weight_stack, col_part))
    weight_stack = exchange_sum(weight_stack, "z")
    self_grad = lax.dot_general(
        grad_pre, self_weight, contract_cols, preferred_element_type=jnp.float32
    )
    present_value = lax.dynamic_slice_in_dim(col_part, row_index * per_device, per_device, 0)
    col_part = lax.dynamic_update_slice_in_dim(
        col_part, present_value + self_grad, row_index * per_device, 0
    )
    y_count = lax.axis_size("y")
    z_count = lax.axis_size("z")
    stage_order = inverse.reshape(y_count, z_count, per_device).transpose(1, 0, 2)
    initial = col_part[stage_order.reshape(-1)].reshape(z_count, y_count, per_device, feature_width)
    initial, weight_stack = lax.optimization_barrier((initial, weight_stack))
    reduced_rows = lax.psum_scatter(initial, "z", scatter_dimension=0, tiled=True)[0]
    weight_stack = exchange_sum(weight_stack, "y")
    reduced_rows, weight_stack = lax.optimization_barrier((reduced_rows, weight_stack))
    reduced_rows = lax.psum_scatter(reduced_rows, "y", scatter_dimension=0, tiled=True)[0]
    grad_features = reduced_rows[None].astype(jnp.bfloat16)
    weight_sums = (
        weight_stack[:feature_width],
        weight_stack[feature_width : 2 * feature_width],
        weight_stack[2 * feature_width],
    )
    return (
        activation[None],
        grad_features,
        weight_sums[0] * grad_scale,
        weight_sums[1] * grad_scale,
        weight_sums[2] * grad_scale,
    )


def torus_split(mesh):
    row_devices = mesh.devices[:, 0]
    try:
        z_count = len({device.coords[2] for device in row_devices})
    except (AttributeError, IndexError, TypeError):
        z_count = 8
    if row_devices.shape[0] % z_count:
        z_count = 1
    return z_count


def solution(mesh):
    z_count = torus_split(mesh)
    y_count = mesh.devices.shape[0] // z_count
    split_mesh = Mesh(mesh.devices.reshape(y_count, z_count, -1), ("y", "z", "col"))
    row = ("y", "z")
    return jax.shard_map(
        on_device,
        mesh=split_mesh,
        in_specs=(
            P("col", row, None),
            P(),
            P(),
            P(),
            P("col", row, None),
            P(row, "col", None, None, None),
            P(row, "col", None),
            P(row, "col", None),
            P(row, "col"),
            P("col", None),
        ),
        out_specs=(P("col", row, None), P("col", row, None), P(), P(), P()),
        check_vma=False,
    )
```

```python
import math

import jax
import jax.numpy as jnp
from jax import lax
from jax.experimental import pallas as pl
from jax.experimental.pallas import tpu as pltpu
from jax.sharding import Mesh, PartitionSpec as P


def tile_forward_kernel(rows_ref, cols_ref, count_ref, tiles_ref, x_ref, out_ref):
    step = pl.program_id(0)
    group, side, _ = tiles_ref.shape

    @pl.when(step == 0)
    def _():
        out_ref[...] = jnp.zeros_like(out_ref)

    for offset in range(group):
        slot = step * group + offset

        @pl.when(slot < count_ref[0])
        def _():
            source = x_ref[pl.ds(pl.multiple_of(cols_ref[slot] * side, side), side), :]
            product = jnp.dot(tiles_ref[offset], source, preferred_element_type=jnp.float32)
            target = pl.ds(pl.multiple_of(rows_ref[slot] * side, side), side)
            out_ref[target, :] = out_ref[target, :] + product


def tile_backward_kernel(rows_ref, cols_ref, count_ref, tiles_ref, s_ref, out_ref):
    step = pl.program_id(0)
    group, side, _ = tiles_ref.shape

    @pl.when(step == 0)
    def _():
        out_ref[...] = jnp.zeros_like(out_ref)

    for offset in range(group):
        slot = step * group + offset

        @pl.when(slot < count_ref[0])
        def _():
            source = s_ref[pl.ds(pl.multiple_of(rows_ref[slot] * side, side), side), :]
            product = lax.dot_general(
                tiles_ref[offset], source, (((0,), (0,)), ((), ())),
                preferred_element_type=jnp.float32,
            )
            target = pl.ds(pl.multiple_of(cols_ref[slot] * side, side), side)
            out_ref[target, :] = out_ref[target, :] + product


def tile_product(kernel, tiles, rows, cols, count, source, out_rows, interpret=False):
    slots, side, _ = tiles.shape
    group = 8 if slots % 8 == 0 else 1
    width = source.shape[1]
    grid_spec = pltpu.PrefetchScalarGridSpec(
        num_scalar_prefetch=3,
        grid=(slots // group,),
        in_specs=[
            pl.BlockSpec((group, side, side), lambda s, r, c, n: (s, 0, 0)),
            pl.BlockSpec(source.shape, lambda s, r, c, n: (0, 0)),
        ],
        out_specs=pl.BlockSpec((out_rows, width), lambda s, r, c, n: (0, 0)),
    )
    return pl.pallas_call(
        kernel,
        grid_spec=grid_spec,
        out_shape=jax.ShapeDtypeStruct((out_rows, width), jnp.float32),
        interpret=interpret,
    )(rows, cols, count, tiles, source)


def exchange_sum(value, axis):
    size = lax.axis_size(axis)
    if size & (size - 1):
        return lax.psum(value, axis)
    distance = 1
    while distance < size:
        pairs = [(index, index ^ distance) for index in range(size)]
        value = value + lax.ppermute(value, axis, pairs)
        distance *= 2
    return value


def halving_sum(value, axis):
    size = lax.axis_size(axis)
    index = lax.axis_index(axis)
    distance = 1
    while distance < size:
        half = value.shape[0] // 2
        upper_side = (index // distance) % 2 == 1
        send = jnp.where(upper_side, value[:half], value[half:])
        keep = jnp.where(upper_side, value[half:], value[:half])
        pairs = [(position, position ^ distance) for position in range(size)]
        value = keep + lax.ppermute(send, axis, pairs)
        distance *= 2
    return value


def doubling_gather(value, axis):
    size = lax.axis_size(axis)
    index = lax.axis_index(axis)
    distance = size // 2
    while distance >= 1:
        pairs = [(position, position ^ distance) for position in range(size)]
        other = lax.ppermute(value, axis, pairs)
        upper_side = (index // distance) % 2 == 1
        value = jnp.where(
            upper_side, jnp.concatenate([other, value]), jnp.concatenate([value, other])
        )
        distance //= 2
    return value


def block_onehot(block_ids, block_total, live_mask):
    targets = jnp.arange(block_total, dtype=jnp.int32)
    return (block_ids[:, None] == targets[None, :]).astype(jnp.float32) * live_mask[:, None]


def on_device(
    features,
    self_weight,
    neighbour_weight,
    bias_term,
    cotangent,
    tile_values,
    tile_rows,
    tile_cols,
    tile_count,
    reorder,
):
    row_count = lax.axis_size("y") * lax.axis_size("z")
    col_count = lax.axis_size("col")
    row_index = lax.axis_index("y") * lax.axis_size("z") + lax.axis_index("z")
    col_index = lax.axis_index("col")
    per_device = features.shape[1]
    feature_width = features.shape[2]
    slot_count = tile_values.shape[2]
    block_side = tile_values.shape[3]
    row_blocks = col_count * per_device // block_side
    col_blocks = row_count * per_device // block_side
    blocks = tile_values[0, 0]
    tile_row_ids = tile_rows[0, 0]
    tile_col_ids = tile_cols[0, 0]
    live_mask = (jnp.arange(slot_count, dtype=jnp.int32) < tile_count[0, 0]).astype(jnp.float32)
    row_pick = block_onehot(tile_row_ids, row_blocks, live_mask)
    order_here = reorder[0]
    maximum_value = lax.Precision.HIGHEST
    contract_rows = (((0,), (0,)), ((), ()))
    contract_cols = (((1,), (1,)), ((), ()))
    row_weight = jnp.sum(blocks, axis=2, dtype=jnp.float32)
    degree_part = lax.dot_general(
        row_pick, row_weight, contract_rows, precision=maximum_value
    ).reshape(col_count, per_device)
    inverse = (
        jnp.zeros_like(order_here)
        .at[order_here]
        .set(jnp.arange(order_here.shape[0], dtype=jnp.int32))
    )
    gathered = lax.all_gather(features, ("y", "z"), axis=1, tiled=True)[0]
    gathered, inverse = lax.optimization_barrier((gathered, inverse))
    ordered = gathered[order_here]
    live_count = tile_count[0].reshape(1)
    partial_value = tile_product(
        tile_forward_kernel, blocks, tile_row_ids, tile_col_ids, live_count, ordered,
        row_blocks * block_side,
    )
    partial_value = partial_value.reshape(col_count, per_device, feature_width)
    degree_rows = jnp.zeros((col_count, 8, feature_width), jnp.float32)
    degree_rows = degree_rows.at[:, 0, :per_device].set(degree_part)
    partial_value = jnp.concatenate([partial_value, degree_rows], axis=1)
    reduced = lax.psum_scatter(partial_value, "col", scatter_dimension=0, tiled=True)[0]
    summed_result = reduced[:per_device]
    degree_own = reduced[per_device, :per_device]
    rescale = lax.rsqrt(1.0 + degree_own)
    aggregate = (summed_result * rescale[:, None]).astype(jnp.bfloat16)
    own_positions = lax.dynamic_slice_in_dim(order_here, row_index * per_device, per_device)
    own_rows = gathered[own_positions]
    preact = jnp.dot(own_rows, self_weight, preferred_element_type=jnp.float32)
    preact = preact + jnp.dot(aggregate, neighbour_weight, preferred_element_type=jnp.float32)
    preact = preact + bias_term.astype(jnp.float32)[None, :]
    sigmoid_value = jax.nn.sigmoid(preact)
    activation = (preact * sigmoid_value).astype(jnp.bfloat16)
    slope = sigmoid_value * (1.0 + preact * (1.0 - sigmoid_value))
    grad_pre = (cotangent[0].astype(jnp.float32) * slope).astype(jnp.bfloat16)
    grad_scale = 1.0 / math.sqrt(per_device * row_count * col_count)
    spread = (
        lax.dot_general(
            grad_pre, neighbour_weight, contract_cols, preferred_element_type=jnp.float32
        )
        * rescale[:, None]
    ).astype(jnp.bfloat16)
    spread_rows = lax.all_gather(spread[None], "col", axis=0, tiled=True).reshape(
        row_blocks, block_side, feature_width
    )
    bias_rows = jnp.zeros((8, feature_width), jnp.float32)
    bias_rows = bias_rows.at[0].set(jnp.sum(grad_pre.astype(jnp.float32), axis=0))
    weight_stack = jnp.concatenate(
        [
            lax.dot_general(own_rows, grad_pre, contract_rows, preferred_element_type=jnp.float32),
            lax.dot_general(aggregate, grad_pre, contract_rows, preferred_element_type=jnp.float32),
            bias_rows,
        ],
        axis=0,
    )
    weight_stack = exchange_sum(weight_stack, "col")
    weight_stack, spread_rows = lax.optimization_barrier((weight_stack, spread_rows))
    col_part = tile_product(
        tile_backward_kernel, blocks, tile_row_ids, tile_col_ids, live_count,
        spread_rows.reshape(row_blocks * block_side, feature_width), col_blocks * block_side,
    )
    col_part = col_part.reshape(row_count * per_device, feature_width)
    weight_stack, col_part = lax.optimization_barrier((weight_stack, col_part))
    z_size = lax.axis_size("z")
    stack_rows = weight_stack.shape[0]
    halving = z_size & (z_size - 1) == 0
    if halving:
        padded_rows = -(-stack_rows // (8 * z_size)) * 8 * z_size
        weight_stack = jnp.pad(weight_stack, ((0, padded_rows - stack_rows), (0, 0)))
        weight_stack = halving_sum(weight_stack, "z")
    else:
        weight_stack = lax.psum(weight_stack, "z")
    self_grad = lax.dot_general(
        grad_pre, self_weight, contract_cols, preferred_element_type=jnp.float32
    )
    present_value = lax.dynamic_slice_in_dim(col_part, row_index * per_device, per_device, 0)
    col_part = lax.dynamic_update_slice_in_dim(
        col_part, present_value + self_grad, row_index * per_device, 0
    )
    y_count = lax.axis_size("y")
    z_count = lax.axis_size("z")
    stage_order = inverse.reshape(y_count, z_count, per_device).transpose(1, 0, 2)
    initial = col_part[stage_order.reshape(-1)].reshape(z_count, y_count, per_device, feature_width)
    initial, weight_stack = lax.optimization_barrier((initial, weight_stack))
    reduced_rows = lax.psum_scatter(initial, "z", scatter_dimension=0, tiled=True)[0]
    weight_stack = exchange_sum(weight_stack, "y")
    reduced_rows, weight_stack = lax.optimization_barrier((reduced_rows, weight_stack))
    reduced_rows = lax.psum_scatter(reduced_rows, "y", scatter_dimension=0, tiled=True)[0]
    if halving:
        weight_stack = doubling_gather(weight_stack, "z")[:stack_rows]
    grad_features = reduced_rows[None].astype(jnp.bfloat16)
    weight_sums = (
        weight_stack[:feature_width],
        weight_stack[feature_width : 2 * feature_width],
        weight_stack[2 * feature_width],
    )
    return (
        activation[None],
        grad_features,
        weight_sums[0] * grad_scale,
        weight_sums[1] * grad_scale,
        weight_sums[2] * grad_scale,
    )


def torus_split(mesh):
    row_devices = mesh.devices[:, 0]
    try:
        z_count = len({device.coords[2] for device in row_devices})
    except (AttributeError, IndexError, TypeError):
        z_count = 8
    if row_devices.shape[0] % z_count:
        z_count = 1
    return z_count


def solution(mesh):
    z_count = torus_split(mesh)
    y_count = mesh.devices.shape[0] // z_count
    split_mesh = Mesh(mesh.devices.reshape(y_count, z_count, -1), ("y", "z", "col"))
    row = ("y", "z")
    return jax.shard_map(
        on_device,
        mesh=split_mesh,
        in_specs=(
            P("col", row, None),
            P(),
            P(),
            P(),
            P("col", row, None),
            P(row, "col", None, None, None),
            P(row, "col", None),
            P(row, "col", None),
            P(row, "col"),
            P("col", None),
        ),
        out_specs=(P("col", row, None), P("col", row, None), P(), P(), P()),
        check_vma=False,
    )
```

```python
import math

import jax
import jax.numpy as jnp
from jax import lax
from jax.experimental import pallas as pl
from jax.experimental.pallas import tpu as pltpu
from jax.sharding import Mesh, PartitionSpec as P


def tile_forward_kernel(rows_ref, cols_ref, count_ref, tiles_ref, x_ref, out_ref):
    step = pl.program_id(0)
    group, side, _ = tiles_ref.shape

    @pl.when(step == 0)
    def _():
        out_ref[...] = jnp.zeros_like(out_ref)

    for offset in range(group):
        slot = step * group + offset

        @pl.when(slot < count_ref[0])
        def _():
            source = x_ref[pl.ds(pl.multiple_of(cols_ref[slot] * side, side), side), :]
            product = jnp.dot(tiles_ref[offset], source, preferred_element_type=jnp.float32)
            target = pl.ds(pl.multiple_of(rows_ref[slot] * side, side), side)
            out_ref[target, :] = out_ref[target, :] + product


def tile_backward_kernel(rows_ref, cols_ref, count_ref, tiles_ref, s_ref, out_ref):
    step = pl.program_id(0)
    group, side, _ = tiles_ref.shape

    @pl.when(step == 0)
    def _():
        out_ref[...] = jnp.zeros_like(out_ref)

    for offset in range(group):
        slot = step * group + offset

        @pl.when(slot < count_ref[0])
        def _():
            source = s_ref[pl.ds(pl.multiple_of(rows_ref[slot] * side, side), side), :]
            product = lax.dot_general(
                tiles_ref[offset], source, (((0,), (0,)), ((), ())),
                preferred_element_type=jnp.float32,
            )
            target = pl.ds(pl.multiple_of(cols_ref[slot] * side, side), side)
            out_ref[target, :] = out_ref[target, :] + product


def tile_product(kernel, tiles, rows, cols, count, source, out_rows, interpret=False):
    slots, side, _ = tiles.shape
    group = 8 if slots % 8 == 0 else 1
    width = source.shape[1]
    grid_spec = pltpu.PrefetchScalarGridSpec(
        num_scalar_prefetch=3,
        grid=(slots // group,),
        in_specs=[
            pl.BlockSpec((group, side, side), lambda s, r, c, n: (s, 0, 0)),
            pl.BlockSpec(source.shape, lambda s, r, c, n: (0, 0)),
        ],
        out_specs=pl.BlockSpec((out_rows, width), lambda s, r, c, n: (0, 0)),
    )
    return pl.pallas_call(
        kernel,
        grid_spec=grid_spec,
        out_shape=jax.ShapeDtypeStruct((out_rows, width), jnp.float32),
        interpret=interpret,
    )(rows, cols, count, tiles, source)


def exchange_sum(value, axis):
    size = lax.axis_size(axis)
    if size & (size - 1):
        return lax.psum(value, axis)
    distance = 1
    while distance < size:
        pairs = [(index, index ^ distance) for index in range(size)]
        value = value + lax.ppermute(value, axis, pairs)
        distance *= 2
    return value


def halving_sum(value, axis):
    size = lax.axis_size(axis)
    index = lax.axis_index(axis)
    distance = 1
    while distance < size:
        half = value.shape[0] // 2
        upper_side = (index // distance) % 2 == 1
        send = jnp.where(upper_side, value[:half], value[half:])
        keep = jnp.where(upper_side, value[half:], value[:half])
        pairs = [(position, position ^ distance) for position in range(size)]
        value = keep + lax.ppermute(send, axis, pairs)
        distance *= 2
    return value


def doubling_gather(value, axis):
    size = lax.axis_size(axis)
    index = lax.axis_index(axis)
    distance = size // 2
    while distance >= 1:
        pairs = [(position, position ^ distance) for position in range(size)]
        other = lax.ppermute(value, axis, pairs)
        upper_side = (index // distance) % 2 == 1
        value = jnp.where(
            upper_side, jnp.concatenate([other, value]), jnp.concatenate([value, other])
        )
        distance //= 2
    return value


def block_onehot(block_ids, block_total, live_mask):
    targets = jnp.arange(block_total, dtype=jnp.int32)
    return (block_ids[:, None] == targets[None, :]).astype(jnp.float32) * live_mask[:, None]


def on_device(
    features,
    self_weight,
    neighbour_weight,
    bias_term,
    cotangent,
    tile_values,
    tile_rows,
    tile_cols,
    tile_count,
    reorder,
):
    row_count = lax.axis_size("y") * lax.axis_size("z")
    col_count = lax.axis_size("col")
    row_index = lax.axis_index("y") * lax.axis_size("z") + lax.axis_index("z")
    col_index = lax.axis_index("col")
    per_device = features.shape[1]
    feature_width = features.shape[2]
    slot_count = tile_values.shape[2]
    block_side = tile_values.shape[3]
    row_blocks = col_count * per_device // block_side
    col_blocks = row_count * per_device // block_side
    blocks = tile_values[0, 0]
    tile_row_ids = tile_rows[0, 0]
    tile_col_ids = tile_cols[0, 0]
    live_mask = (jnp.arange(slot_count, dtype=jnp.int32) < tile_count[0, 0]).astype(jnp.float32)
    row_pick = block_onehot(tile_row_ids, row_blocks, live_mask)
    order_here = reorder[0]
    maximum_value = lax.Precision.HIGHEST
    contract_rows = (((0,), (0,)), ((), ()))
    contract_cols = (((1,), (1,)), ((), ()))
    row_weight = jnp.sum(blocks, axis=2, dtype=jnp.float32)
    degree_part = lax.dot_general(
        row_pick, row_weight, contract_rows, precision=maximum_value
    ).reshape(col_count, per_device)
    inverse = (
        jnp.zeros_like(order_here)
        .at[order_here]
        .set(jnp.arange(order_here.shape[0], dtype=jnp.int32))
    )
    gathered = lax.all_gather(features, ("y", "z"), axis=1, tiled=True)[0]
    gathered, inverse = lax.optimization_barrier((gathered, inverse))
    ordered = gathered[order_here]
    live_count = tile_count[0].reshape(1)
    partial_value = tile_product(
        tile_forward_kernel, blocks, tile_row_ids, tile_col_ids, live_count, ordered,
        row_blocks * block_side,
    )
    partial_value = partial_value.reshape(col_count, per_device, feature_width)
    degree_rows = jnp.zeros((col_count, 8, feature_width), jnp.float32)
    degree_rows = degree_rows.at[:, 0, :per_device].set(degree_part)
    partial_value = jnp.concatenate([partial_value, degree_rows], axis=1)
    reduced = lax.psum_scatter(partial_value, "col", scatter_dimension=0, tiled=True)[0]
    summed_result = reduced[:per_device]
    degree_own = reduced[per_device, :per_device]
    rescale = lax.rsqrt(1.0 + degree_own)
    aggregate = (summed_result * rescale[:, None]).astype(jnp.bfloat16)
    own_positions = lax.dynamic_slice_in_dim(order_here, row_index * per_device, per_device)
    own_rows = gathered[own_positions]
    preact = jnp.dot(own_rows, self_weight, preferred_element_type=jnp.float32)
    preact = preact + jnp.dot(aggregate, neighbour_weight, preferred_element_type=jnp.float32)
    preact = preact + bias_term.astype(jnp.float32)[None, :]
    sigmoid_value = jax.nn.sigmoid(preact)
    activation = (preact * sigmoid_value).astype(jnp.bfloat16)
    slope = sigmoid_value * (1.0 + preact * (1.0 - sigmoid_value))
    grad_pre = (cotangent[0].astype(jnp.float32) * slope).astype(jnp.bfloat16)
    grad_scale = 1.0 / math.sqrt(per_device * row_count * col_count)
    spread = (
        lax.dot_general(
            grad_pre, neighbour_weight, contract_cols, preferred_element_type=jnp.float32
        )
        * rescale[:, None]
    ).astype(jnp.bfloat16)
    spread_rows = lax.all_gather(spread[None], "col", axis=0, tiled=True).reshape(
        row_blocks, block_side, feature_width
    )
    bias_rows = jnp.zeros((8, feature_width), jnp.float32)
    bias_rows = bias_rows.at[0].set(jnp.sum(grad_pre.astype(jnp.float32), axis=0))
    weight_stack = jnp.concatenate(
        [
            lax.dot_general(own_rows, grad_pre, contract_rows, preferred_element_type=jnp.float32),
            lax.dot_general(aggregate, grad_pre, contract_rows, preferred_element_type=jnp.float32),
            bias_rows,
        ],
        axis=0,
    )
    weight_stack = exchange_sum(weight_stack, "col")
    weight_stack, spread_rows = lax.optimization_barrier((weight_stack, spread_rows))
    col_part = tile_product(
        tile_backward_kernel, blocks, tile_row_ids, tile_col_ids, live_count,
        spread_rows.reshape(row_blocks * block_side, feature_width), col_blocks * block_side,
    )
    col_part = col_part.reshape(row_count * per_device, feature_width)
    z_size = lax.axis_size("z")
    stack_rows = weight_stack.shape[0]
    halving = z_size & (z_size - 1) == 0
    if halving:
        padded_rows = -(-stack_rows // (8 * z_size)) * 8 * z_size
        weight_stack = jnp.pad(weight_stack, ((0, padded_rows - stack_rows), (0, 0)))
        weight_stack = halving_sum(weight_stack, "z")
    else:
        weight_stack = lax.psum(weight_stack, "z")
    self_grad = lax.dot_general(
        grad_pre, self_weight, contract_cols, preferred_element_type=jnp.float32
    )
    present_value = lax.dynamic_slice_in_dim(col_part, row_index * per_device, per_device, 0)
    col_part = lax.dynamic_update_slice_in_dim(
        col_part, present_value + self_grad, row_index * per_device, 0
    )
    y_count = lax.axis_size("y")
    z_count = lax.axis_size("z")
    stage_order = inverse.reshape(y_count, z_count, per_device).transpose(1, 0, 2)
    initial = col_part[stage_order.reshape(-1)].reshape(z_count, y_count, per_device, feature_width)
    initial, weight_stack = lax.optimization_barrier((initial, weight_stack))
    reduced_rows = lax.psum_scatter(initial, "z", scatter_dimension=0, tiled=True)[0]
    weight_stack = exchange_sum(weight_stack, "y")
    reduced_rows, weight_stack = lax.optimization_barrier((reduced_rows, weight_stack))
    reduced_rows = lax.psum_scatter(reduced_rows, "y", scatter_dimension=0, tiled=True)[0]
    if halving:
        weight_stack = doubling_gather(weight_stack, "z")[:stack_rows]
    grad_features = reduced_rows[None].astype(jnp.bfloat16)
    weight_sums = (
        weight_stack[:feature_width],
        weight_stack[feature_width : 2 * feature_width],
        weight_stack[2 * feature_width],
    )
    return (
        activation[None],
        grad_features,
        weight_sums[0] * grad_scale,
        weight_sums[1] * grad_scale,
        weight_sums[2] * grad_scale,
    )


def torus_split(mesh):
    row_devices = mesh.devices[:, 0]
    try:
        z_count = len({device.coords[2] for device in row_devices})
    except (AttributeError, IndexError, TypeError):
        z_count = 8
    if row_devices.shape[0] % z_count:
        z_count = 1
    return z_count


def solution(mesh):
    z_count = torus_split(mesh)
    y_count = mesh.devices.shape[0] // z_count
    split_mesh = Mesh(mesh.devices.reshape(y_count, z_count, -1), ("y", "z", "col"))
    row = ("y", "z")
    return jax.shard_map(
        on_device,
        mesh=split_mesh,
        in_specs=(
            P("col", row, None),
            P(),
            P(),
            P(),
            P("col", row, None),
            P(row, "col", None, None, None),
            P(row, "col", None),
            P(row, "col", None),
            P(row, "col"),
            P("col", None),
        ),
        out_specs=(P("col", row, None), P("col", row, None), P(), P(), P()),
        check_vma=False,
    )
```

```python
import math

import jax
import jax.numpy as jnp
from jax import lax
from jax.experimental import pallas as pl
from jax.experimental.pallas import tpu as pltpu
from jax.sharding import Mesh, PartitionSpec as P


def tile_forward_kernel(rows_ref, cols_ref, count_ref, tiles_ref, x_ref, out_ref):
    step = pl.program_id(0)
    group, side, _ = tiles_ref.shape

    @pl.when(step == 0)
    def _():
        out_ref[...] = jnp.zeros_like(out_ref)

    for offset in range(group):
        slot = step * group + offset

        @pl.when(slot < count_ref[0])
        def _():
            source = x_ref[pl.ds(pl.multiple_of(cols_ref[slot] * side, side), side), :]
            product = jnp.dot(tiles_ref[offset], source, preferred_element_type=jnp.float32)
            target = pl.ds(pl.multiple_of(rows_ref[slot] * side, side), side)
            out_ref[target, :] = out_ref[target, :] + product


def tile_backward_kernel(rows_ref, cols_ref, count_ref, tiles_ref, s_ref, out_ref):
    step = pl.program_id(0)
    group, side, _ = tiles_ref.shape

    @pl.when(step == 0)
    def _():
        out_ref[...] = jnp.zeros_like(out_ref)

    for offset in range(group):
        slot = step * group + offset

        @pl.when(slot < count_ref[0])
        def _():
            source = s_ref[pl.ds(pl.multiple_of(rows_ref[slot] * side, side), side), :]
            product = lax.dot_general(
                tiles_ref[offset], source, (((0,), (0,)), ((), ())),
                preferred_element_type=jnp.float32,
            )
            target = pl.ds(pl.multiple_of(cols_ref[slot] * side, side), side)
            out_ref[target, :] = out_ref[target, :] + product


def tile_product(kernel, tiles, rows, cols, count, source, out_rows, interpret=False):
    slots, side, _ = tiles.shape
    group = 8 if slots % 8 == 0 else 1
    width = source.shape[1]
    grid_spec = pltpu.PrefetchScalarGridSpec(
        num_scalar_prefetch=3,
        grid=(slots // group,),
        in_specs=[
            pl.BlockSpec((group, side, side), lambda s, r, c, n: (s, 0, 0)),
            pl.BlockSpec(source.shape, lambda s, r, c, n: (0, 0)),
        ],
        out_specs=pl.BlockSpec((out_rows, width), lambda s, r, c, n: (0, 0)),
    )
    return pl.pallas_call(
        kernel,
        grid_spec=grid_spec,
        out_shape=jax.ShapeDtypeStruct((out_rows, width), jnp.float32),
        interpret=interpret,
    )(rows, cols, count, tiles, source)


def exchange_sum(value, axis):
    size = lax.axis_size(axis)
    if size & (size - 1):
        return lax.psum(value, axis)
    distance = 1
    while distance < size:
        pairs = [(index, index ^ distance) for index in range(size)]
        value = value + lax.ppermute(value, axis, pairs)
        distance *= 2
    return value


def halving_sum(value, axis):
    size = lax.axis_size(axis)
    index = lax.axis_index(axis)
    distance = 1
    while distance < size:
        half = value.shape[0] // 2
        upper_side = (index // distance) % 2 == 1
        send = jnp.where(upper_side, value[:half], value[half:])
        keep = jnp.where(upper_side, value[half:], value[:half])
        pairs = [(position, position ^ distance) for position in range(size)]
        value = keep + lax.ppermute(send, axis, pairs)
        distance *= 2
    return value


def doubling_gather(value, axis):
    size = lax.axis_size(axis)
    index = lax.axis_index(axis)
    distance = size // 2
    while distance >= 1:
        pairs = [(position, position ^ distance) for position in range(size)]
        other = lax.ppermute(value, axis, pairs)
        upper_side = (index // distance) % 2 == 1
        value = jnp.where(
            upper_side, jnp.concatenate([other, value]), jnp.concatenate([value, other])
        )
        distance //= 2
    return value


def block_onehot(block_ids, block_total, live_mask):
    targets = jnp.arange(block_total, dtype=jnp.int32)
    return (block_ids[:, None] == targets[None, :]).astype(jnp.float32) * live_mask[:, None]


def on_device(
    features,
    self_weight,
    neighbour_weight,
    bias_term,
    cotangent,
    tile_values,
    tile_rows,
    tile_cols,
    tile_count,
    reorder,
):
    row_count = lax.axis_size("y") * lax.axis_size("z")
    col_count = lax.axis_size("col")
    row_index = lax.axis_index("y") * lax.axis_size("z") + lax.axis_index("z")
    col_index = lax.axis_index("col")
    per_device = features.shape[1]
    feature_width = features.shape[2]
    slot_count = tile_values.shape[2]
    block_side = tile_values.shape[3]
    row_blocks = col_count * per_device // block_side
    col_blocks = row_count * per_device // block_side
    blocks = tile_values[0, 0]
    tile_row_ids = tile_rows[0, 0]
    tile_col_ids = tile_cols[0, 0]
    live_mask = (jnp.arange(slot_count, dtype=jnp.int32) < tile_count[0, 0]).astype(jnp.float32)
    row_pick = block_onehot(tile_row_ids, row_blocks, live_mask)
    order_here = reorder[0]
    maximum_value = lax.Precision.HIGHEST
    contract_rows = (((0,), (0,)), ((), ()))
    contract_cols = (((1,), (1,)), ((), ()))
    row_weight = jnp.sum(blocks, axis=2, dtype=jnp.float32)
    degree_part = lax.dot_general(
        row_pick, row_weight, contract_rows, precision=maximum_value
    ).reshape(col_count, per_device)
    inverse = (
        jnp.zeros_like(order_here)
        .at[order_here]
        .set(jnp.arange(order_here.shape[0], dtype=jnp.int32))
    )
    gathered = lax.all_gather(features, ("y", "z"), axis=1, tiled=True)[0]
    gathered, inverse = lax.optimization_barrier((gathered, inverse))
    ordered = gathered[order_here]
    live_count = tile_count[0].reshape(1)
    partial_value = tile_product(
        tile_forward_kernel, blocks, tile_row_ids, tile_col_ids, live_count, ordered,
        row_blocks * block_side,
    )
    partial_value = partial_value.reshape(col_count, per_device, feature_width)
    degree_rows = jnp.zeros((col_count, 8, feature_width), jnp.float32)
    degree_rows = degree_rows.at[:, 0, :per_device].set(degree_part)
    partial_value = jnp.concatenate([partial_value, degree_rows], axis=1)
    reduced = lax.psum_scatter(partial_value, "col", scatter_dimension=0, tiled=True)[0]
    summed_result = reduced[:per_device]
    degree_own = reduced[per_device, :per_device]
    rescale = lax.rsqrt(1.0 + degree_own)
    aggregate = (summed_result * rescale[:, None]).astype(jnp.bfloat16)
    own_positions = lax.dynamic_slice_in_dim(order_here, row_index * per_device, per_device)
    own_rows = gathered[own_positions]
    preact = jnp.dot(own_rows, self_weight, preferred_element_type=jnp.float32)
    preact = preact + jnp.dot(aggregate, neighbour_weight, preferred_element_type=jnp.float32)
    preact = preact + bias_term.astype(jnp.float32)[None, :]
    sigmoid_value = jax.nn.sigmoid(preact)
    activation = (preact * sigmoid_value).astype(jnp.bfloat16)
    slope = sigmoid_value * (1.0 + preact * (1.0 - sigmoid_value))
    grad_pre = (cotangent[0].astype(jnp.float32) * slope).astype(jnp.bfloat16)
    grad_scale = 1.0 / math.sqrt(per_device * row_count * col_count)
    spread = (
        lax.dot_general(
            grad_pre, neighbour_weight, contract_cols, preferred_element_type=jnp.float32
        )
        * rescale[:, None]
    ).astype(jnp.bfloat16)
    spread_rows = lax.all_gather(spread[None], "col", axis=0, tiled=True).reshape(
        row_blocks, block_side, feature_width
    )
    bias_rows = jnp.zeros((8, feature_width), jnp.float32)
    bias_rows = bias_rows.at[0].set(jnp.sum(grad_pre.astype(jnp.float32), axis=0))
    weight_stack = jnp.concatenate(
        [
            lax.dot_general(own_rows, grad_pre, contract_rows, preferred_element_type=jnp.float32),
            lax.dot_general(aggregate, grad_pre, contract_rows, preferred_element_type=jnp.float32),
            bias_rows,
        ],
        axis=0,
    )
    z_size = lax.axis_size("z")
    stack_rows = weight_stack.shape[0]
    halving = z_size & (z_size - 1) == 0
    if halving:
        padded_rows = -(-stack_rows // (8 * z_size)) * 8 * z_size
        weight_stack = jnp.pad(weight_stack, ((0, padded_rows - stack_rows), (0, 0)))
        weight_stack = halving_sum(weight_stack, "z")
    else:
        weight_stack = lax.psum(weight_stack, "z")
    weight_stack, spread_rows = lax.optimization_barrier((weight_stack, spread_rows))
    weight_stack = exchange_sum(weight_stack, "col")
    col_part = tile_product(
        tile_backward_kernel, blocks, tile_row_ids, tile_col_ids, live_count,
        spread_rows.reshape(row_blocks * block_side, feature_width), col_blocks * block_side,
    )
    col_part = col_part.reshape(row_count * per_device, feature_width)
    self_grad = lax.dot_general(
        grad_pre, self_weight, contract_cols, preferred_element_type=jnp.float32
    )
    present_value = lax.dynamic_slice_in_dim(col_part, row_index * per_device, per_device, 0)
    col_part = lax.dynamic_update_slice_in_dim(
        col_part, present_value + self_grad, row_index * per_device, 0
    )
    y_count = lax.axis_size("y")
    z_count = lax.axis_size("z")
    stage_order = inverse.reshape(y_count, z_count, per_device).transpose(1, 0, 2)
    initial = col_part[stage_order.reshape(-1)].reshape(z_count, y_count, per_device, feature_width)
    initial, weight_stack = lax.optimization_barrier((initial, weight_stack))
    reduced_rows = lax.psum_scatter(initial, "z", scatter_dimension=0, tiled=True)[0]
    weight_stack = exchange_sum(weight_stack, "y")
    reduced_rows, weight_stack = lax.optimization_barrier((reduced_rows, weight_stack))
    reduced_rows = lax.psum_scatter(reduced_rows, "y", scatter_dimension=0, tiled=True)[0]
    if halving:
        weight_stack = doubling_gather(weight_stack, "z")[:stack_rows]
    grad_features = reduced_rows[None].astype(jnp.bfloat16)
    weight_sums = (
        weight_stack[:feature_width],
        weight_stack[feature_width : 2 * feature_width],
        weight_stack[2 * feature_width],
    )
    return (
        activation[None],
        grad_features,
        weight_sums[0] * grad_scale,
        weight_sums[1] * grad_scale,
        weight_sums[2] * grad_scale,
    )


def torus_split(mesh):
    row_devices = mesh.devices[:, 0]
    try:
        z_count = len({device.coords[2] for device in row_devices})
    except (AttributeError, IndexError, TypeError):
        z_count = 8
    if row_devices.shape[0] % z_count:
        z_count = 1
    return z_count


def solution(mesh):
    z_count = torus_split(mesh)
    y_count = mesh.devices.shape[0] // z_count
    split_mesh = Mesh(mesh.devices.reshape(y_count, z_count, -1), ("y", "z", "col"))
    row = ("y", "z")
    return jax.shard_map(
        on_device,
        mesh=split_mesh,
        in_specs=(
            P("col", row, None),
            P(),
            P(),
            P(),
            P("col", row, None),
            P(row, "col", None, None, None),
            P(row, "col", None),
            P(row, "col", None),
            P(row, "col"),
            P("col", None),
        ),
        out_specs=(P("col", row, None), P("col", row, None), P(), P(), P()),
        check_vma=False,
    )
```

```python
import math

import jax
import jax.numpy as jnp
from jax import lax
from jax.experimental import pallas as pl
from jax.experimental.pallas import tpu as pltpu
from jax.sharding import Mesh, PartitionSpec as P


def tile_forward_kernel(rows_ref, cols_ref, count_ref, tiles_ref, x_ref, out_ref):
    step = pl.program_id(0)
    group, side, _ = tiles_ref.shape

    @pl.when(step == 0)
    def _():
        out_ref[...] = jnp.zeros_like(out_ref)

    for offset in range(group):
        slot = step * group + offset

        @pl.when(slot < count_ref[0])
        def _():
            source = x_ref[pl.ds(pl.multiple_of(cols_ref[slot] * side, side), side), :]
            product = jnp.dot(tiles_ref[offset], source, preferred_element_type=jnp.float32)
            target = pl.ds(pl.multiple_of(rows_ref[slot] * side, side), side)
            out_ref[target, :] = out_ref[target, :] + product


def tile_backward_kernel(rows_ref, cols_ref, count_ref, tiles_ref, s_ref, out_ref):
    step = pl.program_id(0)
    group, side, _ = tiles_ref.shape

    @pl.when(step == 0)
    def _():
        out_ref[...] = jnp.zeros_like(out_ref)

    for offset in range(group):
        slot = step * group + offset

        @pl.when(slot < count_ref[0])
        def _():
            source = s_ref[pl.ds(pl.multiple_of(rows_ref[slot] * side, side), side), :]
            product = lax.dot_general(
                tiles_ref[offset], source, (((0,), (0,)), ((), ())),
                preferred_element_type=jnp.float32,
            )
            target = pl.ds(pl.multiple_of(cols_ref[slot] * side, side), side)
            out_ref[target, :] = out_ref[target, :] + product


def tile_product(kernel, tiles, rows, cols, count, source, out_rows, interpret=False):
    slots, side, _ = tiles.shape
    group = 16 if slots % 16 == 0 else 1
    width = source.shape[1]
    grid_spec = pltpu.PrefetchScalarGridSpec(
        num_scalar_prefetch=3,
        grid=(slots // group,),
        in_specs=[
            pl.BlockSpec((group, side, side), lambda s, r, c, n: (s, 0, 0)),
            pl.BlockSpec(source.shape, lambda s, r, c, n: (0, 0)),
        ],
        out_specs=pl.BlockSpec((out_rows, width), lambda s, r, c, n: (0, 0)),
    )
    return pl.pallas_call(
        kernel,
        grid_spec=grid_spec,
        out_shape=jax.ShapeDtypeStruct((out_rows, width), jnp.float32),
        interpret=interpret,
    )(rows, cols, count, tiles, source)


def exchange_sum(value, axis):
    size = lax.axis_size(axis)
    if size & (size - 1):
        return lax.psum(value, axis)
    distance = 1
    while distance < size:
        pairs = [(index, index ^ distance) for index in range(size)]
        value = value + lax.ppermute(value, axis, pairs)
        distance *= 2
    return value


def halving_sum(value, axis):
    size = lax.axis_size(axis)
    index = lax.axis_index(axis)
    distance = 1
    while distance < size:
        half = value.shape[0] // 2
        upper_side = (index // distance) % 2 == 1
        send = jnp.where(upper_side, value[:half], value[half:])
        keep = jnp.where(upper_side, value[half:], value[:half])
        pairs = [(position, position ^ distance) for position in range(size)]
        value = keep + lax.ppermute(send, axis, pairs)
        distance *= 2
    return value


def doubling_gather(value, axis):
    size = lax.axis_size(axis)
    index = lax.axis_index(axis)
    distance = size // 2
    while distance >= 1:
        pairs = [(position, position ^ distance) for position in range(size)]
        other = lax.ppermute(value, axis, pairs)
        upper_side = (index // distance) % 2 == 1
        value = jnp.where(
            upper_side, jnp.concatenate([other, value]), jnp.concatenate([value, other])
        )
        distance //= 2
    return value


def block_onehot(block_ids, block_total, live_mask):
    targets = jnp.arange(block_total, dtype=jnp.int32)
    return (block_ids[:, None] == targets[None, :]).astype(jnp.float32) * live_mask[:, None]


def on_device(
    features,
    self_weight,
    neighbour_weight,
    bias_term,
    cotangent,
    tile_values,
    tile_rows,
    tile_cols,
    tile_count,
    reorder,
):
    row_count = lax.axis_size("y") * lax.axis_size("z")
    col_count = lax.axis_size("col")
    row_index = lax.axis_index("y") * lax.axis_size("z") + lax.axis_index("z")
    col_index = lax.axis_index("col")
    per_device = features.shape[1]
    feature_width = features.shape[2]
    slot_count = tile_values.shape[2]
    block_side = tile_values.shape[3]
    row_blocks = col_count * per_device // block_side
    col_blocks = row_count * per_device // block_side
    blocks = tile_values[0, 0]
    tile_row_ids = tile_rows[0, 0]
    tile_col_ids = tile_cols[0, 0]
    live_mask = (jnp.arange(slot_count, dtype=jnp.int32) < tile_count[0, 0]).astype(jnp.float32)
    row_pick = block_onehot(tile_row_ids, row_blocks, live_mask)
    order_here = reorder[0]
    maximum_value = lax.Precision.HIGHEST
    contract_rows = (((0,), (0,)), ((), ()))
    contract_cols = (((1,), (1,)), ((), ()))
    row_weight = jnp.sum(blocks, axis=2, dtype=jnp.float32)
    degree_part = lax.dot_general(
        row_pick, row_weight, contract_rows, precision=maximum_value
    ).reshape(col_count, per_device)
    inverse = (
        jnp.zeros_like(order_here)
        .at[order_here]
        .set(jnp.arange(order_here.shape[0], dtype=jnp.int32))
    )
    gathered = lax.all_gather(features, ("y", "z"), axis=1, tiled=True)[0]
    gathered, inverse = lax.optimization_barrier((gathered, inverse))
    ordered = gathered[order_here]
    live_count = tile_count[0].reshape(1)
    partial_value = tile_product(
        tile_forward_kernel, blocks, tile_row_ids, tile_col_ids, live_count, ordered,
        row_blocks * block_side,
    )
    partial_value = partial_value.reshape(col_count, per_device, feature_width)
    degree_rows = jnp.zeros((col_count, 8, feature_width), jnp.float32)
    degree_rows = degree_rows.at[:, 0, :per_device].set(degree_part)
    partial_value = jnp.concatenate([partial_value, degree_rows], axis=1)
    reduced = lax.psum_scatter(partial_value, "col", scatter_dimension=0, tiled=True)[0]
    summed_result = reduced[:per_device]
    degree_own = reduced[per_device, :per_device]
    rescale = lax.rsqrt(1.0 + degree_own)
    aggregate = (summed_result * rescale[:, None]).astype(jnp.bfloat16)
    own_positions = lax.dynamic_slice_in_dim(order_here, row_index * per_device, per_device)
    own_rows = gathered[own_positions]
    preact = jnp.dot(own_rows, self_weight, preferred_element_type=jnp.float32)
    preact = preact + jnp.dot(aggregate, neighbour_weight, preferred_element_type=jnp.float32)
    preact = preact + bias_term.astype(jnp.float32)[None, :]
    sigmoid_value = jax.nn.sigmoid(preact)
    activation = (preact * sigmoid_value).astype(jnp.bfloat16)
    slope = sigmoid_value * (1.0 + preact * (1.0 - sigmoid_value))
    grad_pre = (cotangent[0].astype(jnp.float32) * slope).astype(jnp.bfloat16)
    grad_scale = 1.0 / math.sqrt(per_device * row_count * col_count)
    spread = (
        lax.dot_general(
            grad_pre, neighbour_weight, contract_cols, preferred_element_type=jnp.float32
        )
        * rescale[:, None]
    ).astype(jnp.bfloat16)
    spread_rows = lax.all_gather(spread[None], "col", axis=0, tiled=True).reshape(
        row_blocks, block_side, feature_width
    )
    bias_rows = jnp.zeros((8, feature_width), jnp.float32)
    bias_rows = bias_rows.at[0].set(jnp.sum(grad_pre.astype(jnp.float32), axis=0))
    weight_stack = jnp.concatenate(
        [
            lax.dot_general(own_rows, grad_pre, contract_rows, preferred_element_type=jnp.float32),
            lax.dot_general(aggregate, grad_pre, contract_rows, preferred_element_type=jnp.float32),
            bias_rows,
        ],
        axis=0,
    )
    z_size = lax.axis_size("z")
    stack_rows = weight_stack.shape[0]
    halving = z_size & (z_size - 1) == 0
    if halving:
        padded_rows = -(-stack_rows // (8 * z_size)) * 8 * z_size
        weight_stack = jnp.pad(weight_stack, ((0, padded_rows - stack_rows), (0, 0)))
        weight_stack = halving_sum(weight_stack, "z")
    else:
        weight_stack = lax.psum(weight_stack, "z")
    weight_stack, spread_rows = lax.optimization_barrier((weight_stack, spread_rows))
    weight_stack = exchange_sum(weight_stack, "col")
    col_part = tile_product(
        tile_backward_kernel, blocks, tile_row_ids, tile_col_ids, live_count,
        spread_rows.reshape(row_blocks * block_side, feature_width), col_blocks * block_side,
    )
    col_part = col_part.reshape(row_count * per_device, feature_width)
    self_grad = lax.dot_general(
        grad_pre, self_weight, contract_cols, preferred_element_type=jnp.float32
    )
    present_value = lax.dynamic_slice_in_dim(col_part, row_index * per_device, per_device, 0)
    col_part = lax.dynamic_update_slice_in_dim(
        col_part, present_value + self_grad, row_index * per_device, 0
    )
    y_count = lax.axis_size("y")
    z_count = lax.axis_size("z")
    stage_order = inverse.reshape(y_count, z_count, per_device).transpose(1, 0, 2)
    initial = col_part[stage_order.reshape(-1)].reshape(z_count, y_count, per_device, feature_width)
    initial, weight_stack = lax.optimization_barrier((initial, weight_stack))
    reduced_rows = lax.psum_scatter(initial, "z", scatter_dimension=0, tiled=True)[0]
    weight_stack = exchange_sum(weight_stack, "y")
    reduced_rows, weight_stack = lax.optimization_barrier((reduced_rows, weight_stack))
    reduced_rows = lax.psum_scatter(reduced_rows, "y", scatter_dimension=0, tiled=True)[0]
    if halving:
        weight_stack = doubling_gather(weight_stack, "z")[:stack_rows]
    grad_features = reduced_rows[None].astype(jnp.bfloat16)
    weight_sums = (
        weight_stack[:feature_width],
        weight_stack[feature_width : 2 * feature_width],
        weight_stack[2 * feature_width],
    )
    return (
        activation[None],
        grad_features,
        weight_sums[0] * grad_scale,
        weight_sums[1] * grad_scale,
        weight_sums[2] * grad_scale,
    )


def torus_split(mesh):
    row_devices = mesh.devices[:, 0]
    try:
        z_count = len({device.coords[2] for device in row_devices})
    except (AttributeError, IndexError, TypeError):
        z_count = 8
    if row_devices.shape[0] % z_count:
        z_count = 1
    return z_count


def solution(mesh):
    z_count = torus_split(mesh)
    y_count = mesh.devices.shape[0] // z_count
    split_mesh = Mesh(mesh.devices.reshape(y_count, z_count, -1), ("y", "z", "col"))
    row = ("y", "z")
    return jax.shard_map(
        on_device,
        mesh=split_mesh,
        in_specs=(
            P("col", row, None),
            P(),
            P(),
            P(),
            P("col", row, None),
            P(row, "col", None, None, None),
            P(row, "col", None),
            P(row, "col", None),
            P(row, "col"),
            P("col", None),
        ),
        out_specs=(P("col", row, None), P("col", row, None), P(), P(), P()),
        check_vma=False,
    )
```
